256 devices in a mesh: section: 4 (over y), fsdp: 64 (over z, x, core).
Axes of the slice: x: 4, y: 4, z: 8, core: 2. Of those that a mesh axis runs over, the one named last changes fastest.
Arguments:
- acts: bfloat16 [4, 8192, 4096], P('section', 'fsdp'), may hold values from -6 to 6
- out_grad: bfloat16 [4, 8192, 1024], P('section', 'fsdp'), may hold values from -6 to 6
- norm_gain: float32 [4, 4096], P('section'), may hold values from 0.25 to 1.75
- tiles: bfloat16 [4, 512, 4096], P('section', 'fsdp'), may hold values from -0.25 to 0.25
- tile_cols: int32 [4, 64, 8], P('section'), may hold values from 0 to 15, as said below
- tile_count: int32 [4, 64], P('section'), may hold values from 3 to 8, as said below
- tile_store_slot: int32 [4, 512], P('section'), may hold values from 0 to 511, each once within a row
Outputs:
- handed: bfloat16 [4, 8192, 4096], P('section', 'fsdp')
- weight_grad: float32 [4, 512, 4096], P('section', 'fsdp')
The draws below stay inside these ranges and needn't reach their ends.
Inputs may be any that keep to these rules, and one draw needn't show every extreme that they name: `tile_cols`: within a row panel the listed block columns are all different. `tile_count`: every section has a panel with exactly 8 and a panel with exactly 3 kept tiles. `tile_store_slot`: each section's row is a permutation of the slots.
All inputs are finite; a program needn't handle non-finite values.
Results may differ from the reference program's by a relative error of at most 0.0029.
Values may be sent and summed in bfloat16 or wider, within the bound.
No kernel may reach another device: no remote copies, remote signals or barrier semaphores. Data moves between devices by JAX's collectives and lax.ppermute only.
A program may use at most 128 MiB of HBM per device.

```python
import jax
import jax.numpy as jnp
from jax import lax

DIN = 4096
KV = 1024
TILE_SIDE = 64
MOST_KEPT = 8
PANELS = 64
NCOL = 16
STORE_SLOTS = 512
TOKENS = 8192
N_SECTION = 4


def draw_tile_cols(key, part):
    keys = jax.random.split(key, N_SECTION * PANELS)
    orders = jax.vmap(lambda single: jax.random.permutation(single, NCOL))(keys)
    return orders[:, :MOST_KEPT].reshape(N_SECTION, PANELS, MOST_KEPT).astype(jnp.int32)


def draw_tile_count(key, part):
    base = jax.random.randint(jax.random.fold_in(key, 11), (N_SECTION, PANELS), 3, MOST_KEPT + 1)
    top_panel = jax.random.randint(jax.random.fold_in(key, 12), (N_SECTION,), 0, PANELS)
    step_off = jax.random.randint(jax.random.fold_in(key, 13), (N_SECTION,), 1, PANELS)
    low_panel = (top_panel + step_off) % PANELS
    panel_ids = jnp.arange(PANELS)[None, :]
    base = jnp.where(panel_ids == top_panel[:, None], MOST_KEPT, base)
    base = jnp.where(panel_ids == low_panel[:, None], 3, base)
    return base.astype(jnp.int32)


def steps_of(rng, shape, shards, smallest, top_value):
    def one(dim, blocks):
        draws = jax.random.uniform(jax.random.fold_in(jax.random.fold_in(rng, 6), dim), (blocks,), jnp.float32, smallest / len(shards), top_value / len(shards))
        return jnp.repeat(jnp.exp(draws), shape[dim] // blocks).reshape((-1,) + (1,) * (len(shape) - dim - 1))

    level = one(*shards[0])
    for cut in shards[1:]:
        level = level * one(*cut)
    return level


def gaussian(key, extent, scale, bound, shards=(), kind=jnp.bfloat16):
    gain = steps_of(key, extent, shards, -0.22, 0.18) if shards else 1.0
    array = jax.random.normal(key, extent, jnp.float32) * scale * gain
    return jnp.minimum(jnp.maximum(array, -bound), bound).astype(kind)


def setup_inputs(seed: int = 0) -> dict:
    arg_keys = jax.random.split(jax.random.key(seed), 8)
    acts = gaussian(arg_keys[0], (N_SECTION, TOKENS, DIN), 1.0, 6.0, ((0, 4), (1, 64)))
    out_grad = gaussian(arg_keys[1], (N_SECTION, TOKENS, KV), 1.0, 6.0, ((0, 4), (1, 64)))
    norm_gain = jnp.clip(1.0 + 0.15 * jax.random.normal(arg_keys[2], (N_SECTION, DIN), jnp.float32), 0.25, 1.75)
    tiles = gaussian(arg_keys[3], (N_SECTION, STORE_SLOTS, TILE_SIDE * TILE_SIDE), (MOST_KEPT * TILE_SIDE) ** -0.5, 0.25, ((0, 4), (1, 64)))
    tile_cols = draw_tile_cols(jax.random.fold_in(arg_keys[7], 71), 0)
    tile_count = draw_tile_count(jax.random.fold_in(arg_keys[7], 71), 0)
    tile_store_slot = jax.vmap(lambda own: jax.random.permutation(own, STORE_SLOTS))(jax.random.split(arg_keys[6], N_SECTION)).reshape((N_SECTION, STORE_SLOTS)).astype(jnp.int32)
    return dict(acts=acts, out_grad=out_grad, norm_gain=norm_gain, tiles=tiles, tile_cols=tile_cols, tile_count=tile_count, tile_store_slot=tile_store_slot)


EPS = 1e-05

def one_section(items):
    acts_s, ograd_s, gain_s, tiles_s, cols_s, count_s, section_slots = items
    inputs_f = acts_s.astype(jnp.float32)
    mean_sq = lax.optimization_barrier(jnp.mean(inputs_f * inputs_f, axis=1, keepdims=True))
    recip = lax.rsqrt(mean_sq + EPS)
    normed = (inputs_f * recip * gain_s[None, :]).astype(jnp.bfloat16)
    kept = jnp.arange(MOST_KEPT)[None, :] < count_s[:, None]
    slot_lookup = section_slots.reshape(PANELS, MOST_KEPT)
    placed = tiles_s[slot_lookup]
    placed = jnp.where(kept[:, :, None], placed, jnp.zeros_like(placed))
    placed = placed.reshape(PANELS, MOST_KEPT, TILE_SIDE, TILE_SIDE)
    panel_ids = jnp.arange(PANELS)[:, None]
    dense = jnp.zeros((PANELS, NCOL, TILE_SIDE, TILE_SIDE), jnp.bfloat16).at[panel_ids, cols_s].set(placed)
    dense = dense.transpose(0, 2, 1, 3).reshape(DIN, KV)
    normed_grad = jnp.dot(ograd_s, dense.T, preferred_element_type=jnp.float32)
    scaled = gain_s[None, :] * normed_grad
    inner = lax.optimization_barrier(jnp.sum(scaled * inputs_f, axis=1, keepdims=True)) / DIN
    input_grad = (recip * scaled - inputs_f * recip ** 3 * inner).astype(jnp.bfloat16)
    full_grad = jnp.dot(normed.T, ograd_s, preferred_element_type=jnp.float32) * TOKENS ** (-0.5)
    grad_blocks = full_grad.reshape(PANELS, TILE_SIDE, NCOL, TILE_SIDE).transpose(0, 2, 1, 3)
    picked_tiles = grad_blocks[panel_ids, cols_s]
    picked_tiles = jnp.where(kept[:, :, None, None], picked_tiles, jnp.zeros_like(picked_tiles))
    picked_tiles = picked_tiles.reshape(PANELS * MOST_KEPT, TILE_SIDE * TILE_SIDE)
    slot_gradient = jnp.zeros((STORE_SLOTS, TILE_SIDE * TILE_SIDE), jnp.float32).at[section_slots].set(picked_tiles)
    return (input_grad, slot_gradient)

def reference(acts, out_grad, norm_gain, tiles, tile_cols, tile_count, tile_store_slot):
    input_grads, weight_grad = lax.map(one_section, (acts, out_grad, norm_gain, tiles, tile_cols, tile_count, tile_store_slot))
    handed = jnp.concatenate([input_grads[1:], jnp.zeros_like(input_grads[:1])], axis=0)
    return (handed, weight_grad)
```

```python
import jax
import jax.numpy as jnp
from jax import lax
from jax.sharding import PartitionSpec as P

EPS = 1e-05


def shifted(value, axis, steps):
    count = lax.axis_size(axis)
    leading, last = (max(0, -steps), min(count, count - steps))
    return lax.ppermute(value, axis, [(source, source + steps) for source in range(leading, last)])


def local(acts, out_grad, norm_gain, tiles, tile_cols, tile_count, tile_store_slot):
    inputs_f = acts[0].astype(jnp.float32)
    key_grad = out_grad[0]
    gain_row = norm_gain[0]
    column_list = tile_cols[0]
    count_list = tile_count[0]
    slot_lookup = tile_store_slot[0]
    tok_rows, width = inputs_f.shape
    kv_width = key_grad.shape[1]
    panel_list, most_kept = column_list.shape
    blk = width // panel_list
    ncol = kv_width // blk
    store_slots = panel_list * most_kept
    area = blk * blk
    slot_dev = tiles.shape[1]
    grad_scale = (tok_rows * lax.axis_size("zx") * lax.axis_size("core")) ** (-0.5)
    tile_positions = jnp.arange(store_slots, dtype=jnp.int32)
    inverse_order = jnp.zeros((store_slots,), jnp.int32).at[slot_lookup].set(tile_positions)
    kept_grid = jnp.arange(most_kept)[None, :] < count_list[:, None]
    mean_sq = jnp.mean(inputs_f * inputs_f, axis=1, keepdims=True)
    recip = lax.rsqrt(mean_sq + EPS)
    normed = (inputs_f * recip * gain_row[None, :]).astype(jnp.bfloat16)
    zx_size = lax.axis_size("zx")
    core_size = lax.axis_size("core")
    gathered = lax.all_gather(tiles[0], "zx", axis=0, tiled=True)
    gathered = lax.all_gather(gathered, "core", axis=0, tiled=True)
    slot_ids = jnp.arange(store_slots, dtype=jnp.int32)
    slot_dev_i = slot_ids // (slot_dev * core_size)
    slot_core = (slot_ids // slot_dev) % core_size
    row_of_slot = slot_core * (zx_size * slot_dev) + slot_dev_i * slot_dev + slot_ids % slot_dev
    placed = gathered[row_of_slot[slot_lookup]].reshape(panel_list, most_kept, blk, blk)
    grad_padded = jnp.concatenate(
        [key_grad.reshape(tok_rows, ncol, blk), jnp.zeros((tok_rows, 1, blk), key_grad.dtype)],
        axis=1,
    )
    safe_cols = jnp.where(kept_grid, column_list, ncol)
    selected = grad_padded[:, safe_cols]
    normed_grad = jnp.einsum(
        "tpkb,pkab->tpa", selected, placed, preferred_element_type=jnp.float32
    ).reshape(tok_rows, width)
    normed_blocks = normed.reshape(tok_rows, panel_list, blk)
    terms_pos = jnp.einsum(
        "tpa,tpkb->pkab", normed_blocks, selected, preferred_element_type=jnp.float32
    )
    terms_pos = (terms_pos * grad_scale).reshape(store_slots, area)
    scaled = gain_row[None, :] * normed_grad
    inner = jnp.sum(scaled * inputs_f, axis=1, keepdims=True) / width
    input_grad = (recip * scaled - inputs_f * recip**3 * inner).astype(jnp.bfloat16)
    order_k = jnp.arange(core_size)[:, None, None]
    order_i = jnp.arange(zx_size)[None, :, None]
    order_j = jnp.arange(slot_dev)[None, None, :]
    rs_order = ((order_i * core_size + order_k) * slot_dev + order_j).reshape(-1)
    weight_grad = lax.psum_scatter(terms_pos[inverse_order[rs_order]], "core", scatter_dimension=0, tiled=True)
    weight_grad = lax.psum_scatter(weight_grad, "zx", scatter_dimension=0, tiled=True)
    handed = shifted(input_grad, "section", -1)
    return (handed[None], weight_grad[None])


def solution(mesh):
    sec, fs = mesh.devices.shape
    mesh = jax.sharding.Mesh(mesh.devices.reshape(sec, fs // 2, 2), ("section", "zx", "core"))
    F = ("zx", "core")
    placed = (
        P("section", F, None),
        P("section", F, None),
        P("section", None),
        P("section", F, None),
        P("section", None, None),
        P("section", None),
        P("section", None),
    )
    return jax.shard_map(
        local,
        mesh=mesh,
        in_specs=placed,
        out_specs=(P("section", F, None), P("section", F, None)),
        check_vma=False,
    )
```

```python
import jax
import jax.numpy as jnp
from jax import lax
from jax.sharding import PartitionSpec as P

EPS = 1e-05
FS = ("z", "x", "core")


def shifted(value, axis, steps):
    count = lax.axis_size(axis)
    leading, last = (max(0, -steps), min(count, count - steps))
    return lax.ppermute(value, axis, [(source, source + steps) for source in range(leading, last)])


def local(acts, out_grad, norm_gain, tiles, tile_cols, tile_count, tile_store_slot):
    inputs_f = acts[0].astype(jnp.float32)
    key_grad = out_grad[0]
    gain_row = norm_gain[0]
    column_list = tile_cols[0]
    count_list = tile_count[0]
    slot_lookup = tile_store_slot[0]
    tok_rows, width = inputs_f.shape
    kv_width = key_grad.shape[1]
    panel_list, most_kept = column_list.shape
    blk = width // panel_list
    ncol = kv_width // blk
    store_slots = panel_list * most_kept
    slot_dev = tiles.shape[1]
    nz, nx, nc = (lax.axis_size(a) for a in FS)
    half = blk // 2
    lanes = 2 * blk
    grad_scale = (tok_rows * nz * nx * nc) ** (-0.5)

    own_tiles = tiles[0].reshape(slot_dev, half, lanes)
    gathered = lax.all_gather(own_tiles, "x", axis=0, tiled=True)
    gathered = lax.all_gather(gathered, "z", axis=0, tiled=True)
    gathered = lax.all_gather(gathered, "core", axis=0, tiled=True)
    slot_ids = jnp.arange(store_slots, dtype=jnp.int32)
    holder = slot_ids // slot_dev
    row_of_slot = (holder % nc) * (nz * nx * slot_dev) + (holder // nc) * slot_dev + slot_ids % slot_dev

    kept_grid = jnp.arange(most_kept)[None, :] < count_list[:, None]
    col_hit = (column_list[:, :, None] == jnp.arange(ncol)[None, None, :]) & kept_grid[:, :, None]
    has_tile = jnp.any(col_hit, axis=1)
    k_of = jnp.argmax(col_hit, axis=1)
    pos_of = jnp.arange(panel_list)[:, None] * most_kept + k_of
    dense_rows = jnp.where(has_tile, row_of_slot[slot_lookup[pos_of]], store_slots)

    mean_sq = jnp.mean(inputs_f * inputs_f, axis=1, keepdims=True)
    recip = lax.rsqrt(mean_sq + EPS)
    normed = (inputs_f * recip * gain_row[None, :]).astype(jnp.bfloat16)

    og_blocks = key_grad.reshape(tok_rows, ncol, blk).transpose(1, 0, 2)
    diag = (jnp.arange(2)[:, None] == jnp.arange(lanes)[None, :] // blk)
    og_wide = jnp.concatenate([og_blocks, og_blocks], axis=2)
    expand = jnp.where(diag[None, None, :, :], og_wide[:, :, None, :], jnp.zeros((), key_grad.dtype))

    normed_pairs = normed.reshape(tok_rows, panel_list, half, 2).transpose(1, 2, 3, 0)
    normed_pairs = normed_pairs.reshape(panel_list, half, 2 * tok_rows)
    expand_k = expand.transpose(0, 2, 1, 3).reshape(ncol, 2 * tok_rows, lanes)
    dense_terms = jnp.einsum("prk,ckl->pcrl", normed_pairs, expand_k, preferred_element_type=jnp.float32)
    dense_terms = dense_terms.reshape(panel_list * ncol, half, lanes)
    inverse_order = jnp.zeros((store_slots,), jnp.int32).at[slot_lookup].set(slot_ids)
    pos = inverse_order
    term_panel = pos // most_kept
    term_kept = (pos % most_kept) < count_list[term_panel]
    term_index = term_panel * ncol + column_list[term_panel, pos % most_kept]
    oc = jnp.arange(nc)[:, None, None, None]
    oz = jnp.arange(nz)[None, :, None, None]
    ox = jnp.arange(nx)[None, None, :, None]
    oj = jnp.arange(slot_dev)[None, None, None, :]
    rs_order = (((oz * nx + ox) * nc + oc) * slot_dev + oj).reshape(-1)
    terms = jnp.where(
        term_kept[rs_order][:, None, None], dense_terms[term_index[rs_order]], jnp.zeros((), jnp.float32)
    )
    weight_grad = lax.psum_scatter(terms, "core", scatter_dimension=0, tiled=True)
    weight_grad = lax.psum_scatter(weight_grad, "z", scatter_dimension=0, tiled=True)
    weight_grad = lax.psum_scatter(weight_grad, "x", scatter_dimension=0, tiled=True)
    weight_grad = (weight_grad * grad_scale).reshape(slot_dev, blk * blk)

    gathered_ext = jnp.concatenate([gathered, jnp.zeros((1, half, lanes), gathered.dtype)], axis=0)
    dense_w = gathered_ext[dense_rows.reshape(-1)].reshape(panel_list, ncol, half, lanes)
    normed_grad = jnp.einsum("cthl,pcrl->tprh", expand, dense_w, preferred_element_type=jnp.float32)
    normed_grad = normed_grad.reshape(tok_rows, width)

    scaled = gain_row[None, :] * normed_grad
    inner = jnp.sum(scaled * inputs_f, axis=1, keepdims=True) / width
    input_grad = (recip * scaled - inputs_f * recip**3 * inner).astype(jnp.bfloat16)
    handed = shifted(input_grad, "section", -1)
    return (handed[None], weight_grad[None])


def solution(mesh):
    sec, fs = mesh.devices.shape
    mesh = jax.sharding.Mesh(mesh.devices.reshape(sec, fs // 8, 4, 2), ("section",) + FS)
    placed = (
        P("section", FS, None),
        P("section", FS, None),
        P("section", None),
        P("section", FS, None),
        P("section", None, None),
        P("section", None),
        P("section", None),
    )
    return jax.shard_map(
        local,
        mesh=mesh,
        in_specs=placed,
        out_specs=(P("section", FS, None), P("section", FS, None)),
        check_vma=False,
    )
```

```python
import jax
import jax.numpy as jnp
from jax import lax
from jax.sharding import PartitionSpec as P

EPS = 1e-05
FS = ("z", "x", "core")


def shifted(value, axis, steps):
    count = lax.axis_size(axis)
    leading, last = (max(0, -steps), min(count, count - steps))
    return lax.ppermute(value, axis, [(source, source + steps) for source in range(leading, last)])


def local(acts, out_grad, norm_gain, tiles, tile_cols, tile_count, tile_store_slot):
    inputs_f = acts[0].astype(jnp.float32)
    key_grad = out_grad[0]
    gain_row = norm_gain[0]
    column_list = tile_cols[0]
    count_list = tile_count[0]
    slot_lookup = tile_store_slot[0]
    tok_rows, width = inputs_f.shape
    kv_width = key_grad.shape[1]
    panel_list, most_kept = column_list.shape
    blk = width // panel_list
    ncol = kv_width // blk
    store_slots = panel_list * most_kept
    slot_dev = tiles.shape[1]
    nz, nx, nc = (lax.axis_size(a) for a in FS)
    half = blk // 2
    lanes = 2 * blk
    grad_scale = (tok_rows * nz * nx * nc) ** (-0.5)

    own_tiles = tiles[0].reshape(slot_dev, half, lanes)
    gathered = lax.all_gather(own_tiles, "x", axis=0, tiled=True)
    gathered = lax.all_gather(gathered, "z", axis=0, tiled=True)
    gathered = lax.all_gather(gathered, "core", axis=0, tiled=True)
    slot_ids = jnp.arange(store_slots, dtype=jnp.int32)

    def row_of(slot):
        holder = slot // slot_dev
        return (holder % nc) * (nz * nx * slot_dev) + (holder // nc) * slot_dev + slot % slot_dev

    kept_grid = jnp.arange(most_kept)[None, :] < count_list[:, None]
    col_hit = (column_list[:, :, None] == jnp.arange(ncol)[None, None, :]) & kept_grid[:, :, None]
    has_tile = jnp.any(col_hit, axis=1)
    hit_rows = jnp.sum(jnp.where(col_hit, row_of(slot_lookup.reshape(panel_list, most_kept))[:, :, None], 0), axis=1)
    dense_rows = hit_rows.reshape(-1)

    mean_sq = jnp.mean(inputs_f * inputs_f, axis=1, keepdims=True)
    recip = lax.rsqrt(mean_sq + EPS)
    normed = (inputs_f * recip * gain_row[None, :]).astype(jnp.bfloat16)

    og_blocks = key_grad.reshape(tok_rows, ncol, blk).transpose(1, 0, 2)
    diag = (jnp.arange(2)[:, None] == jnp.arange(lanes)[None, :] // blk)
    og_wide = jnp.concatenate([og_blocks, og_blocks], axis=2)
    expand = jnp.where(diag[None, None, :, :], og_wide[:, :, None, :], jnp.zeros((), key_grad.dtype))

    normed_pairs = normed.reshape(tok_rows, panel_list, half, 2).transpose(1, 2, 3, 0)
    normed_pairs = normed_pairs.reshape(panel_list, half, 2 * tok_rows)
    expand_k = expand.transpose(0, 2, 1, 3).reshape(ncol, 2 * tok_rows, lanes)
    dense_terms = jnp.dot(
        normed_pairs.reshape(panel_list * half, 2 * tok_rows),
        expand_k.transpose(1, 0, 2).reshape(2 * tok_rows, ncol * lanes),
        preferred_element_type=jnp.float32,
    )
    dense_terms = dense_terms.reshape(panel_list, half, ncol, lanes).transpose(0, 2, 1, 3)
    dense_terms = dense_terms.reshape(panel_list * ncol, half, lanes)
    oc = jnp.arange(nc)[:, None, None, None]
    oz = jnp.arange(nz)[None, :, None, None]
    ox = jnp.arange(nx)[None, None, :, None]
    oj = jnp.arange(slot_dev)[None, None, None, :]
    rs_order = (((oz * nx + ox) * nc + oc) * slot_dev + oj).reshape(-1)
    slot_match = slot_lookup[None, :] == rs_order[:, None]
    pos_panel = jnp.arange(store_slots, dtype=jnp.int32) // most_kept
    pos_index = pos_panel * ncol + column_list.reshape(-1)
    pos_kept = kept_grid.reshape(-1)
    term_index = jnp.sum(jnp.where(slot_match, pos_index[None, :], 0), axis=1)
    term_kept = jnp.any(slot_match & pos_kept[None, :], axis=1)
    terms = jnp.where(term_kept[:, None, None], dense_terms[term_index], jnp.zeros((), jnp.float32))
    terms, gathered = lax.optimization_barrier((terms, gathered))
    weight_grad = lax.psum_scatter(terms, "core", scatter_dimension=0, tiled=True)
    weight_grad = lax.psum_scatter(weight_grad, "z", scatter_dimension=0, tiled=True)
    weight_grad = lax.psum_scatter(weight_grad, "x", scatter_dimension=0, tiled=True)
    weight_grad = (weight_grad * grad_scale).reshape(slot_dev, blk * blk)

    dense_w = jnp.where(
        has_tile.reshape(-1)[:, None, None], gathered[dense_rows], jnp.zeros((), gathered.dtype)
    ).reshape(panel_list, ncol, half, lanes)
    normed_grad = jnp.einsum("cthl,pcrl->tprh", expand, dense_w, preferred_element_type=jnp.float32)
    normed_grad = normed_grad.reshape(tok_rows, width)

    scaled = gain_row[None, :] * normed_grad
    inner = jnp.sum(scaled * inputs_f, axis=1, keepdims=True) / width
    input_grad = (recip * scaled - inputs_f * recip**3 * inner).astype(jnp.bfloat16)
    handed = shifted(input_grad, "section", -1)
    return (handed[None], weight_grad[None])


def solution(mesh):
    sec, fs = mesh.devices.shape
    mesh = jax.sharding.Mesh(mesh.devices.reshape(sec, fs // 8, 4, 2), ("section",) + FS)
    placed = (
        P("section", FS, None),
        P("section", FS, None),
        P("section", None),
        P("section", FS, None),
        P("section", None, None),
        P("section", None),
        P("section", None),
    )
    return jax.shard_map(
        local,
        mesh=mesh,
        in_specs=placed,
        out_specs=(P("section", FS, None), P("section", FS, None)),
        check_vma=False,
    )
```

```python
import jax
import jax.numpy as jnp
from jax import lax
from jax.sharding import PartitionSpec as P

EPS = 1e-05
FS = ("z", "x", "core")


def shifted(value, axis, steps):
    count = lax.axis_size(axis)
    leading, last = (max(0, -steps), min(count, count - steps))
    return lax.ppermute(value, axis, [(source, source + steps) for source in range(leading, last)])


def local(acts, out_grad, norm_gain, tiles, tile_cols, tile_count, tile_store_slot):
    inputs_f = acts[0].astype(jnp.float32)
    key_grad = out_grad[0]
    gain_row = norm_gain[0]
    column_list = tile_cols[0]
    count_list = tile_count[0]
    slot_lookup = tile_store_slot[0]
    tok_rows, width = inputs_f.shape
    kv_width = key_grad.shape[1]
    panel_list, most_kept = column_list.shape
    blk = width // panel_list
    ncol = kv_width // blk
    store_slots = panel_list * most_kept
    slot_dev = tiles.shape[1]
    nz, nx, nc = (lax.axis_size(a) for a in FS)
    half = blk // 2
    lanes = 2 * blk
    grad_scale = (tok_rows * nz * nx * nc) ** (-0.5)

    own_tiles = tiles[0].reshape(slot_dev, half, lanes)
    gathered = lax.all_gather(own_tiles, "x", axis=0, tiled=True)
    gathered = lax.all_gather(gathered, "z", axis=0, tiled=True)
    slot_ids = jnp.arange(store_slots, dtype=jnp.int32)

    def row_of(slot):
        holder = slot // slot_dev
        return (holder % nc) * (nz * nx * slot_dev) + (holder // nc) * slot_dev + slot % slot_dev

    kept_grid = jnp.arange(most_kept)[None, :] < count_list[:, None]
    col_hit = (column_list[:, :, None] == jnp.arange(ncol)[None, None, :]) & kept_grid[:, :, None]
    has_tile = jnp.any(col_hit, axis=1)
    hit_rows = jnp.sum(jnp.where(col_hit, row_of(slot_lookup.reshape(panel_list, most_kept))[:, :, None], 0), axis=1)
    dense_rows = hit_rows.reshape(-1)

    mean_sq = jnp.mean(inputs_f * inputs_f, axis=1, keepdims=True)
    recip = lax.rsqrt(mean_sq + EPS)
    normed = (inputs_f * recip * gain_row[None, :]).astype(jnp.bfloat16)

    og_blocks = key_grad.reshape(tok_rows, ncol, blk).transpose(1, 0, 2)
    diag = (jnp.arange(2)[:, None] == jnp.arange(lanes)[None, :] // blk)
    og_wide = jnp.concatenate([og_blocks, og_blocks], axis=2)
    expand = jnp.where(diag[None, None, :, :], og_wide[:, :, None, :], jnp.zeros((), key_grad.dtype))

    normed_pairs = normed.reshape(tok_rows, panel_list, half, 2).transpose(1, 2, 3, 0)
    normed_pairs = normed_pairs.reshape(panel_list, half, 2 * tok_rows)
    expand_k = expand.transpose(0, 2, 1, 3).reshape(ncol, 2 * tok_rows, lanes)
    normed_pairs = jnp.concatenate([normed_pairs, jnp.zeros((1, half, 2 * tok_rows), normed_pairs.dtype)], axis=0)
    dense_terms = jnp.dot(
        normed_pairs.reshape((panel_list + 1) * half, 2 * tok_rows),
        expand_k.transpose(1, 0, 2).reshape(2 * tok_rows, ncol * lanes),
        preferred_element_type=jnp.float32,
    )
    dense_terms = dense_terms.reshape(panel_list + 1, half, ncol, lanes).transpose(0, 2, 1, 3)
    dense_terms = dense_terms.reshape((panel_list + 1) * ncol, half, lanes)
    oc = jnp.arange(nc)[:, None, None, None]
    oz = jnp.arange(nz)[None, :, None, None]
    ox = jnp.arange(nx)[None, None, :, None]
    oj = jnp.arange(slot_dev)[None, None, None, :]
    rs_order = (((oz * nx + ox) * nc + oc) * slot_dev + oj).reshape(-1)
    slot_match = slot_lookup[None, :] == rs_order[:, None]
    pos_panel = jnp.arange(store_slots, dtype=jnp.int32) // most_kept
    pos_index = pos_panel * ncol + column_list.reshape(-1)
    pos_kept = kept_grid.reshape(-1)
    term_index = jnp.sum(jnp.where(slot_match, pos_index[None, :], 0), axis=1)
    term_kept = jnp.any(slot_match & pos_kept[None, :], axis=1)
    terms = dense_terms[jnp.where(term_kept, term_index, panel_list * ncol)]
    terms, gathered = lax.optimization_barrier((terms, gathered))
    gathered = lax.all_gather(gathered, "core", axis=0, tiled=True)
    weight_grad = lax.psum_scatter(terms, "core", scatter_dimension=0, tiled=True)
    weight_grad = lax.psum_scatter(weight_grad, "z", scatter_dimension=0, tiled=True)
    weight_grad = lax.psum_scatter(weight_grad, "x", scatter_dimension=0, tiled=True)
    weight_grad = (weight_grad * grad_scale).reshape(slot_dev, blk * blk)

    dense_w = jnp.where(
        has_tile.reshape(-1)[:, None, None], gathered[dense_rows], jnp.zeros((), gathered.dtype)
    ).reshape(panel_list, ncol, half, lanes)
    normed_grad = jnp.einsum("cthl,pcrl->tprh", expand, dense_w, preferred_element_type=jnp.float32)
    normed_grad = normed_grad.reshape(tok_rows, width)

    scaled = gain_row[None, :] * normed_grad
    inner = jnp.sum(scaled * inputs_f, axis=1, keepdims=True) / width
    input_grad = (recip * scaled - inputs_f * recip**3 * inner).astype(jnp.bfloat16)
    handed = shifted(input_grad, "section", -1)
    return (handed[None], weight_grad[None])


def solution(mesh):
    sec, fs = mesh.devices.shape
    mesh = jax.sharding.Mesh(mesh.devices.reshape(sec, fs // 8, 4, 2), ("section",) + FS)
    placed = (
        P("section", FS, None),
        P("section", FS, None),
        P("section", None),
        P("section", FS, None),
        P("section", None, None),
        P("section", None),
        P("section", None),
    )
    return jax.shard_map(
        local,
        mesh=mesh,
        in_specs=placed,
        out_specs=(P("section", FS, None), P("section", FS, None)),
        check_vma=False,
    )
```

```python
import jax
import jax.numpy as jnp
from jax import lax
from jax.sharding import PartitionSpec as P

EPS = 1e-05
FS = ("z", "x", "core")


def shifted(value, axis, steps):
    count = lax.axis_size(axis)
    leading, last = (max(0, -steps), min(count, count - steps))
    return lax.ppermute(value, axis, [(source, source + steps) for source in range(leading, last)])


def sibling(value):
    count = lax.axis_size("core")
    return lax.ppermute(value, "core", [(source, (source + 1) % count) for source in range(count)])


def local(acts, out_grad, norm_gain, tiles, tile_cols, tile_count, tile_store_slot):
    inputs_f = acts[0].astype(jnp.float32)
    key_grad = out_grad[0]
    gain_row = norm_gain[0]
    column_list = tile_cols[0]
    count_list = tile_count[0]
    slot_lookup = tile_store_slot[0]
    tok_rows, width = inputs_f.shape
    kv_width = key_grad.shape[1]
    panel_list, most_kept = column_list.shape
    blk = width // panel_list
    ncol = kv_width // blk
    store_slots = panel_list * most_kept
    slot_dev = tiles.shape[1]
    nz, nx, nc = (lax.axis_size(a) for a in FS)
    half = blk // 2
    lanes = 2 * blk
    grad_scale = (tok_rows * nz * nx * nc) ** (-0.5)

    own_tiles = tiles[0].reshape(slot_dev, half, lanes)
    gathered = lax.all_gather(own_tiles, "x", axis=0, tiled=True)
    gathered = lax.all_gather(gathered, "z", axis=0, tiled=True)
    slot_ids = jnp.arange(store_slots, dtype=jnp.int32)

    my_core = lax.axis_index("core")

    def row_of(slot):
        holder = slot // slot_dev
        half_of = (holder % nc - my_core) % nc
        return half_of * (nz * nx * slot_dev) + (holder // nc) * slot_dev + slot % slot_dev

    kept_grid = jnp.arange(most_kept)[None, :] < count_list[:, None]
    col_hit = (column_list[:, :, None] == jnp.arange(ncol)[None, None, :]) & kept_grid[:, :, None]
    has_tile = jnp.any(col_hit, axis=1)
    hit_rows = jnp.sum(jnp.where(col_hit, row_of(slot_lookup.reshape(panel_list, most_kept))[:, :, None], 0), axis=1)
    dense_rows = hit_rows.reshape(-1)

    mean_sq = jnp.mean(inputs_f * inputs_f, axis=1, keepdims=True)
    recip = lax.rsqrt(mean_sq + EPS)
    normed = (inputs_f * recip * gain_row[None, :]).astype(jnp.bfloat16)
    pair_tokens = nc * tok_rows
    normed_pair = jnp.concatenate([normed, sibling(normed)], axis=0)
    og_pair = jnp.concatenate([key_grad, sibling(key_grad)], axis=0)

    og_blocks = key_grad.reshape(tok_rows, ncol, blk).transpose(1, 0, 2)
    diag = (jnp.arange(2)[:, None] == jnp.arange(lanes)[None, :] // blk)
    og_wide = jnp.concatenate([og_blocks, og_blocks], axis=2)
    expand = jnp.where(diag[None, None, :, :], og_wide[:, :, None, :], jnp.zeros((), key_grad.dtype))

    pair_blocks = og_pair.reshape(pair_tokens, ncol, blk).transpose(1, 0, 2)
    pair_wide = jnp.concatenate([pair_blocks, pair_blocks], axis=2)
    expand_pair = jnp.where(diag[None, None, :, :], pair_wide[:, :, None, :], jnp.zeros((), key_grad.dtype))
    normed_pairs = normed_pair.reshape(pair_tokens, panel_list, half, 2).transpose(1, 2, 3, 0)
    normed_pairs = normed_pairs.reshape(panel_list, half, 2 * pair_tokens)
    expand_k = expand_pair.transpose(0, 2, 1, 3).reshape(ncol, 2 * pair_tokens, lanes)
    normed_pairs = jnp.concatenate([normed_pairs, jnp.zeros((1, half, 2 * pair_tokens), normed_pairs.dtype)], axis=0)
    dense_terms = jnp.dot(
        normed_pairs.reshape((panel_list + 1) * half, 2 * pair_tokens),
        expand_k.transpose(1, 0, 2).reshape(2 * pair_tokens, ncol * lanes),
        preferred_element_type=jnp.float32,
    )
    dense_terms = dense_terms.reshape(panel_list + 1, half, ncol, lanes).transpose(0, 2, 1, 3)
    dense_terms = dense_terms.reshape((panel_list + 1) * ncol, half, lanes)
    oz = jnp.arange(nz)[:, None, None]
    ox = jnp.arange(nx)[None, :, None]
    oj = jnp.arange(slot_dev)[None, None, :]
    rs_order = (((oz * nx + ox) * nc + my_core) * slot_dev + oj).reshape(-1)
    slot_match = slot_lookup[None, :] == rs_order[:, None]
    pos_panel = jnp.arange(store_slots, dtype=jnp.int32) // most_kept
    pos_index = pos_panel * ncol + column_list.reshape(-1)
    pos_kept = kept_grid.reshape(-1)
    term_index = jnp.sum(jnp.where(slot_match, pos_index[None, :], 0), axis=1)
    term_kept = jnp.any(slot_match & pos_kept[None, :], axis=1)
    terms = dense_terms[jnp.where(term_kept, term_index, panel_list * ncol)]
    terms, gathered = lax.optimization_barrier((terms, gathered))
    gathered = jnp.concatenate([gathered, sibling(gathered)], axis=0)
    weight_grad = lax.psum_scatter(terms, "z", scatter_dimension=0, tiled=True)
    weight_grad = lax.psum_scatter(weight_grad, "x", scatter_dimension=0, tiled=True)
    weight_grad = (weight_grad * grad_scale).reshape(slot_dev, blk * blk)

    dense_w = jnp.where(
        has_tile.reshape(-1)[:, None, None], gathered[dense_rows], jnp.zeros((), gathered.dtype)
    ).reshape(panel_list, ncol, half, lanes)
    normed_grad = jnp.einsum("cthl,pcrl->tprh", expand, dense_w, preferred_element_type=jnp.float32)
    normed_grad = normed_grad.reshape(tok_rows, width)

    scaled = gain_row[None, :] * normed_grad
    inner = jnp.sum(scaled * inputs_f, axis=1, keepdims=True) / width
    input_grad = (recip * scaled - inputs_f * recip**3 * inner).astype(jnp.bfloat16)
    handed = shifted(input_grad, "section", -1)
    return (handed[None], weight_grad[None])


def solution(mesh):
    sec, fs = mesh.devices.shape
    mesh = jax.sharding.Mesh(mesh.devices.reshape(sec, fs // 8, 4, 2), ("section",) + FS)
    placed = (
        P("section", FS, None),
        P("section", FS, None),
        P("section", None),
        P("section", FS, None),
        P("section", None, None),
        P("section", None),
        P("section", None),
    )
    return jax.shard_map(
        local,
        mesh=mesh,
        in_specs=placed,
        out_specs=(P("section", FS, None), P("section", FS, None)),
        check_vma=False,
    )
```

```python
import jax
import jax.numpy as jnp
from jax import lax
from jax.sharding import PartitionSpec as P

EPS = 1e-05
FS = ("z", "x", "core")


def shifted(value, axis, steps):
    count = lax.axis_size(axis)
    leading, last = (max(0, -steps), min(count, count - steps))
    return lax.ppermute(value, axis, [(source, source + steps) for source in range(leading, last)])


def sibling(value):
    count = lax.axis_size("core")
    return lax.ppermute(value, "core", [(source, (source + 1) % count) for source in range(count)])


def local(acts, out_grad, norm_gain, tiles, tile_cols, tile_count, tile_store_slot):
    inputs_f = acts[0].astype(jnp.float32)
    key_grad = out_grad[0]
    gain_row = norm_gain[0]
    column_list = tile_cols[0]
    count_list = tile_count[0]
    slot_lookup = tile_store_slot[0]
    tok_rows, width = inputs_f.shape
    kv_width = key_grad.shape[1]
    panel_list, most_kept = column_list.shape
    blk = width // panel_list
    ncol = kv_width // blk
    store_slots = panel_list * most_kept
    slot_dev = tiles.shape[1]
    nz, nx, nc = (lax.axis_size(a) for a in FS)
    half = blk // 2
    lanes = 2 * blk
    grad_scale = (tok_rows * nz * nx * nc) ** (-0.5)

    own_tiles = tiles[0].reshape(slot_dev, half, lanes)
    gathered = jnp.concatenate(
        [own_tiles]
        + [lax.ppermute(own_tiles, "x", [(src, (src + s) % nx) for src in range(nx)]) for s in range(1, nx)],
        axis=0,
    )
    gathered = lax.all_gather(gathered, "z", axis=0, tiled=True)
    slot_ids = jnp.arange(store_slots, dtype=jnp.int32)

    my_core = lax.axis_index("core")
    my_x = lax.axis_index("x")

    def row_of(slot):
        holder = slot // slot_dev
        half_of = (holder % nc - my_core) % nc
        chip = holder // nc
        shift = (my_x - chip % nx) % nx
        return half_of * (nz * nx * slot_dev) + ((chip // nx) * nx + shift) * slot_dev + slot % slot_dev

    kept_grid = jnp.arange(most_kept)[None, :] < count_list[:, None]
    col_hit = (column_list[:, :, None] == jnp.arange(ncol)[None, None, :]) & kept_grid[:, :, None]
    has_tile = jnp.any(col_hit, axis=1)
    hit_rows = jnp.sum(jnp.where(col_hit, row_of(slot_lookup.reshape(panel_list, most_kept))[:, :, None], 0), axis=1)
    dense_rows = hit_rows.reshape(-1)

    mean_sq = jnp.mean(inputs_f * inputs_f, axis=1, keepdims=True)
    recip = lax.rsqrt(mean_sq + EPS)
    normed = (inputs_f * recip * gain_row[None, :]).astype(jnp.bfloat16)
    pair_tokens = nc * tok_rows
    normed_pair = jnp.concatenate([normed, sibling(normed)], axis=0)
    og_pair = jnp.concatenate([key_grad, sibling(key_grad)], axis=0)

    og_blocks = key_grad.reshape(tok_rows, ncol, blk).transpose(1, 0, 2)
    diag = (jnp.arange(2)[:, None] == jnp.arange(lanes)[None, :] // blk)
    og_wide = jnp.concatenate([og_blocks, og_blocks], axis=2)
    expand = jnp.where(diag[None, None, :, :], og_wide[:, :, None, :], jnp.zeros((), key_grad.dtype))

    pair_blocks = og_pair.reshape(pair_tokens, ncol, blk).transpose(1, 0, 2)
    pair_wide = jnp.concatenate([pair_blocks, pair_blocks], axis=2)
    expand_pair = jnp.where(diag[None, None, :, :], pair_wide[:, :, None, :], jnp.zeros((), key_grad.dtype))
    normed_pairs = normed_pair.reshape(pair_tokens, panel_list, half, 2).transpose(1, 2, 3, 0)
    normed_pairs = normed_pairs.reshape(panel_list, half, 2 * pair_tokens)
    expand_k = expand_pair.transpose(0, 2, 1, 3).reshape(ncol, 2 * pair_tokens, lanes)
    normed_pairs = jnp.concatenate([normed_pairs, jnp.zeros((1, half, 2 * pair_tokens), normed_pairs.dtype)], axis=0)
    dense_terms = jnp.dot(
        normed_pairs.reshape((panel_list + 1) * half, 2 * pair_tokens),
        expand_k.transpose(1, 0, 2).reshape(2 * pair_tokens, ncol * lanes),
        preferred_element_type=jnp.float32,
    )
    dense_terms = dense_terms.reshape(panel_list + 1, half, ncol, lanes).transpose(0, 2, 1, 3)
    dense_terms = dense_terms.reshape((panel_list + 1) * ncol, half, lanes)
    oz = jnp.arange(nz)[:, None, None]
    ox = jnp.arange(nx)[None, :, None]
    oj = jnp.arange(slot_dev)[None, None, :]
    rs_order = (((oz * nx + ox) * nc + my_core) * slot_dev + oj).reshape(-1)
    slot_match = slot_lookup[None, :] == rs_order[:, None]
    pos_panel = jnp.arange(store_slots, dtype=jnp.int32) // most_kept
    pos_index = pos_panel * ncol + column_list.reshape(-1)
    pos_kept = kept_grid.reshape(-1)
    term_index = jnp.sum(jnp.where(slot_match, pos_index[None, :], 0), axis=1)
    term_kept = jnp.any(slot_match & pos_kept[None, :], axis=1)
    terms = dense_terms[jnp.where(term_kept, term_index, panel_list * ncol)]
    terms, gathered = lax.optimization_barrier((terms, gathered))
    gathered = jnp.concatenate([gathered, sibling(gathered)], axis=0)
    weight_grad = lax.psum_scatter(terms, "z", scatter_dimension=0, tiled=True)
    weight_grad = lax.psum_scatter(weight_grad, "x", scatter_dimension=0, tiled=True)
    weight_grad = (weight_grad * grad_scale).reshape(slot_dev, blk * blk)

    dense_w = jnp.where(
        has_tile.reshape(-1)[:, None, None], gathered[dense_rows], jnp.zeros((), gathered.dtype)
    ).reshape(panel_list, ncol, half, lanes)
    normed_grad = jnp.einsum("cthl,pcrl->tprh", expand, dense_w, preferred_element_type=jnp.float32)
    normed_grad = normed_grad.reshape(tok_rows, width)

    scaled = gain_row[None, :] * normed_grad
    inner = jnp.sum(scaled * inputs_f, axis=1, keepdims=True) / width
    input_grad = (recip * scaled - inputs_f * recip**3 * inner).astype(jnp.bfloat16)
    handed = shifted(input_grad, "section", -1)
    return (handed[None], weight_grad[None])


def solution(mesh):
    sec, fs = mesh.devices.shape
    mesh = jax.sharding.Mesh(mesh.devices.reshape(sec, fs // 8, 4, 2), ("section",) + FS)
    placed = (
        P("section", FS, None),
        P("section", FS, None),
        P("section", None),
        P("section", FS, None),
        P("section", None, None),
        P("section", None),
        P("section", None),
    )
    return jax.shard_map(
        local,
        mesh=mesh,
        in_specs=placed,
        out_specs=(P("section", FS, None), P("section", FS, None)),
        check_vma=False,
    )
```

```python
import jax
import jax.numpy as jnp
from jax import lax
from jax.sharding import PartitionSpec as P

EPS = 1e-05
FS = ("z", "x", "core")


def shifted(value, axis, steps):
    count = lax.axis_size(axis)
    leading, last = (max(0, -steps), min(count, count - steps))
    return lax.ppermute(value, axis, [(source, source + steps) for source in range(leading, last)])


def sibling(value):
    count = lax.axis_size("core")
    return lax.ppermute(value, "core", [(source, (source + 1) % count) for source in range(count)])


def local(acts, out_grad, norm_gain, tiles, tile_cols, tile_count, tile_store_slot):
    inputs_f = acts[0].astype(jnp.float32)
    key_grad = out_grad[0]
    gain_row = norm_gain[0]
    column_list = tile_cols[0]
    count_list = tile_count[0]
    slot_lookup = tile_store_slot[0]
    tok_rows, width = inputs_f.shape
    kv_width = key_grad.shape[1]
    panel_list, most_kept = column_list.shape
    blk = width // panel_list
    ncol = kv_width // blk
    store_slots = panel_list * most_kept
    slot_dev = tiles.shape[1]
    nz, nx, nc = (lax.axis_size(a) for a in FS)
    half = blk // 2
    lanes = 2 * blk
    grad_scale = (tok_rows * nz * nx * nc) ** (-0.5)

    own_tiles = tiles[0].reshape(slot_dev, half, lanes)
    gathered = jnp.concatenate(
        [own_tiles]
        + [lax.ppermute(own_tiles, "x", [(src, (src + s) % nx) for src in range(nx)]) for s in range(1, nx)],
        axis=0,
    )
    gathered = lax.all_gather(gathered, "z", axis=0, tiled=True)
    slot_ids = jnp.arange(store_slots, dtype=jnp.int32)

    my_core = lax.axis_index("core")
    my_x = lax.axis_index("x")

    def row_of(slot):
        holder = slot // slot_dev
        half_of = (holder % nc - my_core) % nc
        chip = holder // nc
        shift = (my_x - chip % nx) % nx
        return half_of * (nz * nx * slot_dev) + ((chip // nx) * nx + shift) * slot_dev + slot % slot_dev

    kept_grid = jnp.arange(most_kept)[None, :] < count_list[:, None]
    col_hit = (column_list[:, :, None] == jnp.arange(ncol)[None, None, :]) & kept_grid[:, :, None]
    has_tile = jnp.any(col_hit, axis=1)
    hit_rows = jnp.sum(jnp.where(col_hit, row_of(slot_lookup.reshape(panel_list, most_kept))[:, :, None], 0), axis=1)
    dense_rows = hit_rows.reshape(-1)

    mean_sq = jnp.mean(inputs_f * inputs_f, axis=1, keepdims=True)
    recip = lax.rsqrt(mean_sq + EPS)
    normed = (inputs_f * recip * gain_row[None, :]).astype(jnp.bfloat16)
    pair_tokens = nc * tok_rows
    normed_pair = jnp.concatenate([normed, sibling(normed)], axis=0)
    og_pair = jnp.concatenate([key_grad, sibling(key_grad)], axis=0)

    og_blocks = key_grad.reshape(tok_rows, ncol, blk).transpose(1, 0, 2)
    diag = (jnp.arange(2)[:, None] == jnp.arange(lanes)[None, :] // blk)
    og_wide = jnp.concatenate([og_blocks, og_blocks], axis=2)
    expand = jnp.where(diag[None, None, :, :], og_wide[:, :, None, :], jnp.zeros((), key_grad.dtype))

    pair_blocks = og_pair.reshape(pair_tokens, ncol, blk).transpose(1, 0, 2)
    pair_wide = jnp.concatenate([pair_blocks, pair_blocks], axis=2)
    expand_pair = jnp.where(diag[None, None, :, :], pair_wide[:, :, None, :], jnp.zeros((), key_grad.dtype))
    normed_pairs = normed_pair.reshape(pair_tokens, panel_list, half, 2).transpose(1, 2, 3, 0)
    normed_pairs = normed_pairs.reshape(panel_list, half, 2 * pair_tokens)
    expand_k = expand_pair.transpose(0, 2, 1, 3).reshape(ncol, 2 * pair_tokens, lanes)
    normed_pairs = jnp.concatenate([normed_pairs, jnp.zeros((1, half, 2 * pair_tokens), normed_pairs.dtype)], axis=0)
    dense_terms = jnp.dot(
        normed_pairs.reshape((panel_list + 1) * half, 2 * pair_tokens),
        expand_k.transpose(1, 0, 2).reshape(2 * pair_tokens, ncol * lanes),
        preferred_element_type=jnp.float32,
    )
    dense_terms = dense_terms.reshape(panel_list + 1, half, ncol, lanes).transpose(0, 2, 1, 3)
    dense_terms = dense_terms.reshape((panel_list + 1) * ncol, half, lanes)
    oz = jnp.arange(nz)[:, None, None]
    ox = jnp.arange(nx)[None, :, None]
    oj = jnp.arange(slot_dev)[None, None, :]
    rs_order = (((oz * nx + ox) * nc + my_core) * slot_dev + oj).reshape(-1)
    slot_match = slot_lookup[None, :] == rs_order[:, None]
    pos_panel = jnp.arange(store_slots, dtype=jnp.int32) // most_kept
    pos_index = pos_panel * ncol + column_list.reshape(-1)
    pos_kept = kept_grid.reshape(-1)
    term_index = jnp.sum(jnp.where(slot_match, pos_index[None, :], 0), axis=1)
    term_kept = jnp.any(slot_match & pos_kept[None, :], axis=1)
    terms = dense_terms[jnp.where(term_kept, term_index, panel_list * ncol)]
    terms, gathered = lax.optimization_barrier((terms, gathered))
    gathered = jnp.concatenate([gathered, sibling(gathered)], axis=0)
    weight_grad = lax.psum_scatter(terms, "z", scatter_dimension=0, tiled=True)
    x_blocks = weight_grad.reshape(nx, slot_dev, half, lanes)
    own_sum = lax.dynamic_index_in_dim(x_blocks, my_x, axis=0, keepdims=False)
    for s in range(1, nx):
        outgoing = lax.dynamic_index_in_dim(x_blocks, (my_x + s) % nx, axis=0, keepdims=False)
        own_sum = own_sum + lax.ppermute(outgoing, "x", [(src, (src + s) % nx) for src in range(nx)])
    weight_grad = own_sum
    weight_grad = (weight_grad * grad_scale).reshape(slot_dev, blk * blk)

    dense_w = jnp.where(
        has_tile.reshape(-1)[:, None, None], gathered[dense_rows], jnp.zeros((), gathered.dtype)
    ).reshape(panel_list, ncol, half, lanes)
    normed_grad = jnp.einsum("cthl,pcrl->tprh", expand, dense_w, preferred_element_type=jnp.float32)
    normed_grad = normed_grad.reshape(tok_rows, width)

    scaled = gain_row[None, :] * normed_grad
    inner = jnp.sum(scaled * inputs_f, axis=1, keepdims=True) / width
    input_grad = (recip * scaled - inputs_f * recip**3 * inner).astype(jnp.bfloat16)
    handed = shifted(input_grad, "section", -1)
    return (handed[None], weight_grad[None])


def solution(mesh):
    sec, fs = mesh.devices.shape
    mesh = jax.sharding.Mesh(mesh.devices.reshape(sec, fs // 8, 4, 2), ("section",) + FS)
    placed = (
        P("section", FS, None),
        P("section", FS, None),
        P("section", None),
        P("section", FS, None),
        P("section", None, None),
        P("section", None),
        P("section", None),
    )
    return jax.shard_map(
        local,
        mesh=mesh,
        in_specs=placed,
        out_specs=(P("section", FS, None), P("section", FS, None)),
        check_vma=False,
    )
```

```python
import jax
import jax.numpy as jnp
from jax import lax
from jax.sharding import PartitionSpec as P

EPS = 1e-05
FS = ("z", "x", "core")


def shifted(value, axis, steps):
    count = lax.axis_size(axis)
    leading, last = (max(0, -steps), min(count, count - steps))
    return lax.ppermute(value, axis, [(source, source + steps) for source in range(leading, last)])


def sibling(value):
    count = lax.axis_size("core")
    return lax.ppermute(value, "core", [(source, (source + 1) % count) for source in range(count)])


def local(acts, out_grad, norm_gain, tiles, tile_cols, tile_count, tile_store_slot):
    inputs_f = acts[0].astype(jnp.float32)
    key_grad = out_grad[0]
    gain_row = norm_gain[0]
    column_list = tile_cols[0]
    count_list = tile_count[0]
    slot_lookup = tile_store_slot[0]
    tok_rows, width = inputs_f.shape
    kv_width = key_grad.shape[1]
    panel_list, most_kept = column_list.shape
    blk = width // panel_list
    ncol = kv_width // blk
    store_slots = panel_list * most_kept
    slot_dev = tiles.shape[1]
    nz, nx, nc = (lax.axis_size(a) for a in FS)
    half = blk // 2
    lanes = 2 * blk
    grad_scale = (tok_rows * nz * nx * nc) ** (-0.5)

    own_tiles = tiles[0].reshape(slot_dev, half, lanes)
    gathered = jnp.concatenate(
        [own_tiles]
        + [lax.ppermute(own_tiles, "x", [(src, (src + s) % nx) for src in range(nx)]) for s in range(1, nx)],
        axis=0,
    )
    gathered = lax.all_gather(gathered, "z", axis=0, tiled=True)
    slot_ids = jnp.arange(store_slots, dtype=jnp.int32)

    my_core = lax.axis_index("core")
    my_x = lax.axis_index("x")

    def row_of(slot):
        holder = slot // slot_dev
        half_of = (holder % nc - my_core) % nc
        chip = holder // nc
        shift = (my_x - chip % nx) % nx
        return half_of * (nz * nx * slot_dev) + ((chip // nx) * nx + shift) * slot_dev + slot % slot_dev

    kept_grid = jnp.arange(most_kept)[None, :] < count_list[:, None]
    col_hit = (column_list[:, :, None] == jnp.arange(ncol)[None, None, :]) & kept_grid[:, :, None]
    has_tile = jnp.any(col_hit, axis=1)
    hit_rows = jnp.sum(jnp.where(col_hit, row_of(slot_lookup.reshape(panel_list, most_kept))[:, :, None], 0), axis=1)
    dense_rows = hit_rows.reshape(-1)

    mean_sq = jnp.mean(inputs_f * inputs_f, axis=1, keepdims=True)
    recip = lax.rsqrt(mean_sq + EPS)
    normed = (inputs_f * recip * gain_row[None, :]).astype(jnp.bfloat16)
    pair_tokens = nc * tok_rows
    normed_pair = jnp.concatenate([normed, sibling(normed)], axis=0)
    og_pair = jnp.concatenate([key_grad, sibling(key_grad)], axis=0)

    og_blocks = key_grad.reshape(tok_rows, ncol, blk).transpose(1, 0, 2)
    diag = (jnp.arange(2)[:, None] == jnp.arange(lanes)[None, :] // blk)
    og_wide = jnp.concatenate([og_blocks, og_blocks], axis=2)
    expand = jnp.where(diag[None, None, :, :], og_wide[:, :, None, :], jnp.zeros((), key_grad.dtype))

    pair_blocks = og_pair.reshape(pair_tokens, ncol, blk).transpose(1, 0, 2)
    pair_wide = jnp.concatenate([pair_blocks, pair_blocks], axis=2)
    expand_pair = jnp.where(diag[None, None, :, :], pair_wide[:, :, None, :], jnp.zeros((), key_grad.dtype))
    normed_pairs = normed_pair.reshape(pair_tokens, panel_list, half, 2).transpose(1, 2, 3, 0)
    normed_pairs = normed_pairs.reshape(panel_list, half, 2 * pair_tokens)
    expand_k = expand_pair.transpose(0, 2, 1, 3).reshape(ncol, 2 * pair_tokens, lanes)
    normed_pairs = jnp.concatenate([normed_pairs, jnp.zeros((1, half, 2 * pair_tokens), normed_pairs.dtype)], axis=0)
    dense_terms = jnp.dot(
        normed_pairs.reshape((panel_list + 1) * half, 2 * pair_tokens),
        expand_k.transpose(1, 0, 2).reshape(2 * pair_tokens, ncol * lanes),
        preferred_element_type=jnp.float32,
    )
    dense_terms = dense_terms.reshape(panel_list + 1, half, ncol, lanes).transpose(0, 2, 1, 3)
    dense_terms = dense_terms.reshape((panel_list + 1) * ncol, half, lanes)
    ox = jnp.arange(nx)[:, None, None]
    oz = jnp.arange(nz)[None, :, None]
    oj = jnp.arange(slot_dev)[None, None, :]
    rs_order = (((oz * nx + ox) * nc + my_core) * slot_dev + oj).reshape(-1)
    slot_match = slot_lookup[None, :] == rs_order[:, None]
    pos_panel = jnp.arange(store_slots, dtype=jnp.int32) // most_kept
    pos_index = pos_panel * ncol + column_list.reshape(-1)
    pos_kept = kept_grid.reshape(-1)
    term_index = jnp.sum(jnp.where(slot_match, pos_index[None, :], 0), axis=1)
    term_kept = jnp.any(slot_match & pos_kept[None, :], axis=1)
    terms = dense_terms[jnp.where(term_kept, term_index, panel_list * ncol)]
    terms, gathered = lax.optimization_barrier((terms, gathered))
    gathered = jnp.concatenate([gathered, sibling(gathered)], axis=0)
    x_blocks = terms.reshape(nx, nz * slot_dev, half, lanes)
    own_sum = lax.dynamic_index_in_dim(x_blocks, my_x, axis=0, keepdims=False)
    for s in range(1, nx):
        outgoing = lax.dynamic_index_in_dim(x_blocks, (my_x + s) % nx, axis=0, keepdims=False)
        own_sum = own_sum + lax.ppermute(outgoing, "x", [(src, (src + s) % nx) for src in range(nx)])
    weight_grad = lax.psum_scatter(own_sum, "z", scatter_dimension=0, tiled=True)
    weight_grad = (weight_grad * grad_scale).reshape(slot_dev, blk * blk)

    dense_w = jnp.where(
        has_tile.reshape(-1)[:, None, None], gathered[dense_rows], jnp.zeros((), gathered.dtype)
    ).reshape(panel_list, ncol, half, lanes)
    normed_grad = jnp.einsum("cthl,pcrl->tprh", expand, dense_w, preferred_element_type=jnp.float32)
    normed_grad = normed_grad.reshape(tok_rows, width)

    scaled = gain_row[None, :] * normed_grad
    inner = jnp.sum(scaled * inputs_f, axis=1, keepdims=True) / width
    input_grad = (recip * scaled - inputs_f * recip**3 * inner).astype(jnp.bfloat16)
    handed = shifted(input_grad, "section", -1)
    return (handed[None], weight_grad[None])


def solution(mesh):
    sec, fs = mesh.devices.shape
    mesh = jax.sharding.Mesh(mesh.devices.reshape(sec, fs // 8, 4, 2), ("section",) + FS)
    placed = (
        P("section", FS, None),
        P("section", FS, None),
        P("section", None),
        P("section", FS, None),
        P("section", None, None),
        P("section", None),
        P("section", None),
    )
    return jax.shard_map(
        local,
        mesh=mesh,
        in_specs=placed,
        out_specs=(P("section", FS, None), P("section", FS, None)),
        check_vma=False,
    )
```

```python
import jax
import jax.numpy as jnp
from jax import lax
from jax.sharding import PartitionSpec as P

EPS = 1e-05
FS = ("z", "x", "core")


def shifted(value, axis, steps):
    count = lax.axis_size(axis)
    leading, last = (max(0, -steps), min(count, count - steps))
    return lax.ppermute(value, axis, [(source, source + steps) for source in range(leading, last)])


def sibling(value):
    count = lax.axis_size("core")
    return lax.ppermute(value, "core", [(source, (source + 1) % count) for source in range(count)])


def local(acts, out_grad, norm_gain, tiles, tile_cols, tile_count, tile_store_slot):
    inputs_f = acts[0].astype(jnp.float32)
    key_grad = out_grad[0]
    gain_row = norm_gain[0]
    column_list = tile_cols[0]
    count_list = tile_count[0]
    slot_lookup = tile_store_slot[0]
    tok_rows, width = inputs_f.shape
    kv_width = key_grad.shape[1]
    panel_list, most_kept = column_list.shape
    blk = width // panel_list
    ncol = kv_width // blk
    store_slots = panel_list * most_kept
    slot_dev = tiles.shape[1]
    nz, nx, nc = (lax.axis_size(a) for a in FS)
    half = blk // 2
    lanes = 2 * blk
    grad_scale = (tok_rows * nz * nx * nc) ** (-0.5)

    own_tiles = tiles[0].reshape(slot_dev, half, lanes)
    my_x = lax.axis_index("x")
    ring4 = nx == 4
    if ring4:
        first = jnp.concatenate([own_tiles, lax.ppermute(own_tiles, "x", [(i, i ^ 1) for i in range(nx)])], axis=0)
        gathered = jnp.concatenate([first, lax.ppermute(first, "x", [(i, nx - 1 - i) for i in range(nx)])], axis=0)
    else:
        gathered = jnp.concatenate(
            [own_tiles]
            + [lax.ppermute(own_tiles, "x", [(src, (src + s) % nx) for src in range(nx)]) for s in range(1, nx)],
            axis=0,
        )
    gathered = lax.all_gather(gathered, "z", axis=0, tiled=True)
    slot_ids = jnp.arange(store_slots, dtype=jnp.int32)

    my_core = lax.axis_index("core")

    def row_of(slot):
        holder = slot // slot_dev
        half_of = (holder % nc - my_core) % nc
        chip = holder // nc
        src_x = chip % nx
        if ring4:
            shift = jnp.where(src_x == my_x, 0, jnp.where(src_x == my_x ^ 1, 1, jnp.where(src_x == nx - 1 - my_x, 2, 3)))
        else:
            shift = (my_x - src_x) % nx
        return half_of * (nz * nx * slot_dev) + ((chip // nx) * nx + shift) * slot_dev + slot % slot_dev

    kept_grid = jnp.arange(most_kept)[None, :] < count_list[:, None]
    col_hit = (column_list[:, :, None] == jnp.arange(ncol)[None, None, :]) & kept_grid[:, :, None]
    has_tile = jnp.any(col_hit, axis=1)
    hit_rows = jnp.sum(jnp.where(col_hit, row_of(slot_lookup.reshape(panel_list, most_kept))[:, :, None], 0), axis=1)
    dense_rows = hit_rows.reshape(-1)

    mean_sq = jnp.mean(inputs_f * inputs_f, axis=1, keepdims=True)
    recip = lax.rsqrt(mean_sq + EPS)
    normed = (inputs_f * recip * gain_row[None, :]).astype(jnp.bfloat16)
    pair_tokens = nc * tok_rows
    normed_pair = jnp.concatenate([normed, sibling(normed)], axis=0)
    og_pair = jnp.concatenate([key_grad, sibling(key_grad)], axis=0)

    og_blocks = key_grad.reshape(tok_rows, ncol, blk).transpose(1, 0, 2)
    diag = (jnp.arange(2)[:, None] == jnp.arange(lanes)[None, :] // blk)
    og_wide = jnp.concatenate([og_blocks, og_blocks], axis=2)
    expand = jnp.where(diag[None, None, :, :], og_wide[:, :, None, :], jnp.zeros((), key_grad.dtype))

    pair_blocks = og_pair.reshape(pair_tokens, ncol, blk).transpose(1, 0, 2)
    pair_wide = jnp.concatenate([pair_blocks, pair_blocks], axis=2)
    expand_pair = jnp.where(diag[None, None, :, :], pair_wide[:, :, None, :], jnp.zeros((), key_grad.dtype))
    normed_pairs = normed_pair.reshape(pair_tokens, panel_list, half, 2).transpose(1, 2, 3, 0)
    normed_pairs = normed_pairs.reshape(panel_list, half, 2 * pair_tokens)
    expand_k = expand_pair.transpose(0, 2, 1, 3).reshape(ncol, 2 * pair_tokens, lanes)
    normed_pairs = jnp.concatenate([normed_pairs, jnp.zeros((1, half, 2 * pair_tokens), normed_pairs.dtype)], axis=0)
    dense_terms = jnp.dot(
        normed_pairs.reshape((panel_list + 1) * half, 2 * pair_tokens),
        expand_k.transpose(1, 0, 2).reshape(2 * pair_tokens, ncol * lanes),
        preferred_element_type=jnp.float32,
    )
    dense_terms = dense_terms.reshape(panel_list + 1, half, ncol, lanes).transpose(0, 2, 1, 3)
    dense_terms = dense_terms.reshape((panel_list + 1) * ncol, half, lanes)
    oz = jnp.arange(nz)[:, None, None]
    ox = jnp.arange(nx)[None, :, None]
    oj = jnp.arange(slot_dev)[None, None, :]
    rs_order = (((oz * nx + ox) * nc + my_core) * slot_dev + oj).reshape(-1)
    slot_match = slot_lookup[None, :] == rs_order[:, None]
    pos_panel = jnp.arange(store_slots, dtype=jnp.int32) // most_kept
    pos_index = pos_panel * ncol + column_list.reshape(-1)
    pos_kept = kept_grid.reshape(-1)
    term_index = jnp.sum(jnp.where(slot_match, pos_index[None, :], 0), axis=1)
    term_kept = jnp.any(slot_match & pos_kept[None, :], axis=1)
    terms = dense_terms[jnp.where(term_kept, term_index, panel_list * ncol)]
    terms, gathered = lax.optimization_barrier((terms, gathered))
    gathered = jnp.concatenate([gathered, sibling(gathered)], axis=0)
    weight_grad = lax.psum_scatter(terms, "z", scatter_dimension=0, tiled=True)
    x_blocks = weight_grad.reshape(nx, slot_dev, half, lanes)

    def block(index):
        return lax.dynamic_index_in_dim(x_blocks, index, axis=0, keepdims=False)

    if ring4:
        pair_x = my_x ^ 1
        sent = jnp.stack([block(pair_x), block(nx - 1 - pair_x)])
        got = lax.ppermute(sent, "x", [(i, i ^ 1) for i in range(nx)])
        keep_own = block(my_x) + got[0]
        keep_far = block(nx - 1 - my_x) + got[1]
        weight_grad = keep_own + lax.ppermute(keep_far, "x", [(i, nx - 1 - i) for i in range(nx)])
    else:
        own_sum = block(my_x)
        for s in range(1, nx):
            own_sum = own_sum + lax.ppermute(block((my_x + s) % nx), "x", [(src, (src + s) % nx) for src in range(nx)])
        weight_grad = own_sum
    weight_grad = (weight_grad * grad_scale).reshape(slot_dev, blk * blk)

    dense_w = jnp.where(
        has_tile.reshape(-1)[:, None, None], gathered[dense_rows], jnp.zeros((), gathered.dtype)
    ).reshape(panel_list, ncol, half, lanes)
    normed_grad = jnp.einsum("cthl,pcrl->tprh", expand, dense_w, preferred_element_type=jnp.float32)
    normed_grad = normed_grad.reshape(tok_rows, width)

    scaled = gain_row[None, :] * normed_grad
    inner = jnp.sum(scaled * inputs_f, axis=1, keepdims=True) / width
    input_grad = (recip * scaled - inputs_f * recip**3 * inner).astype(jnp.bfloat16)
    handed = shifted(input_grad, "section", -1)
    return (handed[None], weight_grad[None])


def solution(mesh):
    sec, fs = mesh.devices.shape
    mesh = jax.sharding.Mesh(mesh.devices.reshape(sec, fs // 8, 4, 2), ("section",) + FS)
    placed = (
        P("section", FS, None),
        P("section", FS, None),
        P("section", None),
        P("section", FS, None),
        P("section", None, None),
        P("section", None),
        P("section", None),
    )
    return jax.shard_map(
        local,
        mesh=mesh,
        in_specs=placed,
        out_specs=(P("section", FS, None), P("section", FS, None)),
        check_vma=False,
    )
```

```python
import jax
import jax.numpy as jnp
from jax import lax
from jax.sharding import PartitionSpec as P

EPS = 1e-05
FS = ("z", "x", "core")


def shifted(value, axis, steps):
    count = lax.axis_size(axis)
    leading, last = (max(0, -steps), min(count, count - steps))
    return lax.ppermute(value, axis, [(source, source + steps) for source in range(leading, last)])


def sibling(value):
    count = lax.axis_size("core")
    return lax.ppermute(value, "core", [(source, (source + 1) % count) for source in range(count)])


def local(acts, out_grad, norm_gain, tiles, tile_cols, tile_count, tile_store_slot):
    inputs_f = acts[0].astype(jnp.float32)
    key_grad = out_grad[0]
    gain_row = norm_gain[0]
    column_list = tile_cols[0]
    count_list = tile_count[0]
    slot_lookup = tile_store_slot[0]
    tok_rows, width = inputs_f.shape
    kv_width = key_grad.shape[1]
    panel_list, most_kept = column_list.shape
    blk = width // panel_list
    ncol = kv_width // blk
    store_slots = panel_list * most_kept
    slot_dev = tiles.shape[1]
    nz, nx, nc = (lax.axis_size(a) for a in FS)
    half = blk // 2
    lanes = 2 * blk
    grad_scale = (tok_rows * nz * nx * nc) ** (-0.5)

    own_tiles = tiles[0].reshape(slot_dev, half, lanes)
    padded = jnp.concatenate([own_tiles, jnp.zeros(((nx - 1) * slot_dev, half, lanes), own_tiles.dtype)], axis=0)
    gathered_z = lax.all_gather(padded, "z", axis=0, tiled=True).reshape(nz, nx * slot_dev, half, lanes)
    gathered_z = gathered_z[:, :slot_dev].reshape(nz * slot_dev, half, lanes)
    slot_ids = jnp.arange(store_slots, dtype=jnp.int32)

    my_core = lax.axis_index("core")
    my_x = lax.axis_index("x")

    def row_of(slot):
        holder = slot // slot_dev
        half_of = (holder % nc - my_core) % nc
        chip = holder // nc
        shift = (my_x - chip % nx) % nx
        return half_of * (nz * nx * slot_dev) + (shift * nz + chip // nx) * slot_dev + slot % slot_dev

    kept_grid = jnp.arange(most_kept)[None, :] < count_list[:, None]
    col_hit = (column_list[:, :, None] == jnp.arange(ncol)[None, None, :]) & kept_grid[:, :, None]
    has_tile = jnp.any(col_hit, axis=1)
    hit_rows = jnp.sum(jnp.where(col_hit, row_of(slot_lookup.reshape(panel_list, most_kept))[:, :, None], 0), axis=1)
    dense_rows = hit_rows.reshape(-1)

    mean_sq = jnp.mean(inputs_f * inputs_f, axis=1, keepdims=True)
    recip = lax.rsqrt(mean_sq + EPS)
    normed = (inputs_f * recip * gain_row[None, :]).astype(jnp.bfloat16)
    pair_tokens = nc * tok_rows
    normed_pair = jnp.concatenate([normed, sibling(normed)], axis=0)
    og_pair = jnp.concatenate([key_grad, sibling(key_grad)], axis=0)

    og_blocks = key_grad.reshape(tok_rows, ncol, blk).transpose(1, 0, 2)
    diag = (jnp.arange(2)[:, None] == jnp.arange(lanes)[None, :] // blk)
    og_wide = jnp.concatenate([og_blocks, og_blocks], axis=2)
    expand = jnp.where(diag[None, None, :, :], og_wide[:, :, None, :], jnp.zeros((), key_grad.dtype))

    pair_blocks = og_pair.reshape(pair_tokens, ncol, blk).transpose(1, 0, 2)
    pair_wide = jnp.concatenate([pair_blocks, pair_blocks], axis=2)
    expand_pair = jnp.where(diag[None, None, :, :], pair_wide[:, :, None, :], jnp.zeros((), key_grad.dtype))
    normed_pairs = normed_pair.reshape(pair_tokens, panel_list, half, 2).transpose(1, 2, 3, 0)
    normed_pairs = normed_pairs.reshape(panel_list, half, 2 * pair_tokens)
    expand_k = expand_pair.transpose(0, 2, 1, 3).reshape(ncol, 2 * pair_tokens, lanes)
    normed_pairs = jnp.concatenate([normed_pairs, jnp.zeros((1, half, 2 * pair_tokens), normed_pairs.dtype)], axis=0)
    dense_terms = jnp.dot(
        normed_pairs.reshape((panel_list + 1) * half, 2 * pair_tokens),
        expand_k.transpose(1, 0, 2).reshape(2 * pair_tokens, ncol * lanes),
        preferred_element_type=jnp.float32,
    )
    dense_terms = dense_terms.reshape(panel_list + 1, half, ncol, lanes).transpose(0, 2, 1, 3)
    dense_terms = dense_terms.reshape((panel_list + 1) * ncol, half, lanes)
    oz = jnp.arange(nz)[:, None, None]
    ox = jnp.arange(nx)[None, :, None]
    oj = jnp.arange(slot_dev)[None, None, :]
    rs_order = (((oz * nx + ox) * nc + my_core) * slot_dev + oj).reshape(-1)
    slot_match = slot_lookup[None, :] == rs_order[:, None]
    pos_panel = jnp.arange(store_slots, dtype=jnp.int32) // most_kept
    pos_index = pos_panel * ncol + column_list.reshape(-1)
    pos_kept = kept_grid.reshape(-1)
    term_index = jnp.sum(jnp.where(slot_match, pos_index[None, :], 0), axis=1)
    term_kept = jnp.any(slot_match & pos_kept[None, :], axis=1)
    terms = dense_terms[jnp.where(term_kept, term_index, panel_list * ncol)]
    terms, gathered_z = lax.optimization_barrier((terms, gathered_z))
    gathered = jnp.concatenate(
        [gathered_z]
        + [lax.ppermute(gathered_z, "x", [(src, (src + s) % nx) for src in range(nx)]) for s in range(1, nx)],
        axis=0,
    )
    gathered = jnp.concatenate([gathered, sibling(gathered)], axis=0)
    weight_grad = lax.psum_scatter(terms, "z", scatter_dimension=0, tiled=True)
    x_blocks = weight_grad.reshape(nx, slot_dev, half, lanes)
    own_sum = lax.dynamic_index_in_dim(x_blocks, my_x, axis=0, keepdims=False)
    for s in range(1, nx):
        outgoing = lax.dynamic_index_in_dim(x_blocks, (my_x + s) % nx, axis=0, keepdims=False)
        own_sum = own_sum + lax.ppermute(outgoing, "x", [(src, (src + s) % nx) for src in range(nx)])
    weight_grad = own_sum
    weight_grad = (weight_grad * grad_scale).reshape(slot_dev, blk * blk)

    dense_w = jnp.where(
        has_tile.reshape(-1)[:, None, None], gathered[dense_rows], jnp.zeros((), gathered.dtype)
    ).reshape(panel_list, ncol, half, lanes)
    normed_grad = jnp.einsum("cthl,pcrl->tprh", expand, dense_w, preferred_element_type=jnp.float32)
    normed_grad = normed_grad.reshape(tok_rows, width)

    scaled = gain_row[None, :] * normed_grad
    inner = jnp.sum(scaled * inputs_f, axis=1, keepdims=True) / width
    input_grad = (recip * scaled - inputs_f * recip**3 * inner).astype(jnp.bfloat16)
    handed = shifted(input_grad, "section", -1)
    return (handed[None], weight_grad[None])


def solution(mesh):
    sec, fs = mesh.devices.shape
    mesh = jax.sharding.Mesh(mesh.devices.reshape(sec, fs // 8, 4, 2), ("section",) + FS)
    placed = (
        P("section", FS, None),
        P("section", FS, None),
        P("section", None),
        P("section", FS, None),
        P("section", None, None),
        P("section", None),
        P("section", None),
    )
    return jax.shard_map(
        local,
        mesh=mesh,
        in_specs=placed,
        out_specs=(P("section", FS, None), P("section", FS, None)),
        check_vma=False,
    )
```

```python
import jax
import jax.numpy as jnp
from jax import lax
from jax.sharding import PartitionSpec as P

EPS = 1e-05
FS = ("z", "x", "core")


def shifted(value, axis, steps):
    count = lax.axis_size(axis)
    leading, last = (max(0, -steps), min(count, count - steps))
    return lax.ppermute(value, axis, [(source, source + steps) for source in range(leading, last)])


def sibling(value):
    count = lax.axis_size("core")
    return lax.ppermute(value, "core", [(source, (source + 1) % count) for source in range(count)])


def local(acts, out_grad, norm_gain, tiles, tile_cols, tile_count, tile_store_slot):
    inputs_f = acts[0].astype(jnp.float32)
    key_grad = out_grad[0]
    gain_row = norm_gain[0]
    column_list = tile_cols[0]
    count_list = tile_count[0]
    slot_lookup = tile_store_slot[0]
    tok_rows, width = inputs_f.shape
    kv_width = key_grad.shape[1]
    panel_list, most_kept = column_list.shape
    blk = width // panel_list
    ncol = kv_width // blk
    store_slots = panel_list * most_kept
    slot_dev = tiles.shape[1]
    nz, nx, nc = (lax.axis_size(a) for a in FS)
    half = blk // 2
    lanes = 2 * blk
    grad_scale = (tok_rows * nz * nx * nc) ** (-0.5)

    own_tiles = tiles[0].reshape(slot_dev, half, lanes)
    gathered = jnp.concatenate(
        [own_tiles]
        + [lax.ppermute(own_tiles, "x", [(src, (src + s) % nx) for src in range(nx)]) for s in range(1, nx)],
        axis=0,
    )
    gathered = lax.all_gather(gathered, "z", axis=0, tiled=True)
    slot_ids = jnp.arange(store_slots, dtype=jnp.int32)

    my_core = lax.axis_index("core")
    my_x = lax.axis_index("x")

    def row_of(slot):
        holder = slot // slot_dev
        half_of = (holder % nc - my_core) % nc
        chip = holder // nc
        shift = (my_x - chip % nx) % nx
        return half_of * (nz * nx * slot_dev) + ((chip // nx) * nx + shift) * slot_dev + slot % slot_dev

    kept_grid = jnp.arange(most_kept)[None, :] < count_list[:, None]
    col_hit = (column_list[:, :, None] == jnp.arange(ncol)[None, None, :]) & kept_grid[:, :, None]
    has_tile = jnp.any(col_hit, axis=1)
    hit_rows = jnp.sum(jnp.where(col_hit, row_of(slot_lookup.reshape(panel_list, most_kept))[:, :, None], 0), axis=1)
    dense_rows = hit_rows.reshape(-1)

    mean_sq = jnp.mean(inputs_f * inputs_f, axis=1, keepdims=True)
    recip = lax.rsqrt(mean_sq + EPS)
    normed = (inputs_f * recip * gain_row[None, :]).astype(jnp.bfloat16)
    pair_tokens = nc * tok_rows
    normed_pair = jnp.concatenate([normed, sibling(normed)], axis=0)
    og_pair = jnp.concatenate([key_grad, sibling(key_grad)], axis=0)

    og_blocks = key_grad.reshape(tok_rows, ncol, blk).transpose(1, 0, 2)
    diag = (jnp.arange(2)[:, None] == jnp.arange(lanes)[None, :] // blk)
    og_wide = jnp.concatenate([og_blocks, og_blocks], axis=2)
    expand = jnp.where(diag[None, None, :, :], og_wide[:, :, None, :], jnp.zeros((), key_grad.dtype))

    pair_blocks = og_pair.reshape(pair_tokens, ncol, blk).transpose(1, 0, 2)
    pair_wide = jnp.concatenate([pair_blocks, pair_blocks], axis=2)
    expand_pair = jnp.where(diag[None, None, :, :], pair_wide[:, :, None, :], jnp.zeros((), key_grad.dtype))
    normed_pairs = normed_pair.reshape(pair_tokens, panel_list, half, 2).transpose(1, 2, 3, 0)
    normed_pairs = normed_pairs.reshape(panel_list, half, 2 * pair_tokens)
    expand_k = expand_pair.transpose(0, 2, 1, 3).reshape(ncol, 2 * pair_tokens, lanes)
    normed_pairs = jnp.concatenate([normed_pairs, jnp.zeros((1, half, 2 * pair_tokens), normed_pairs.dtype)], axis=0)
    dense_terms = jnp.dot(
        normed_pairs.reshape((panel_list + 1) * half, 2 * pair_tokens),
        expand_k.transpose(1, 0, 2).reshape(2 * pair_tokens, ncol * lanes),
        preferred_element_type=jnp.float32,
    )
    dense_terms = dense_terms.reshape(panel_list + 1, half, ncol, lanes).transpose(0, 2, 1, 3)
    dense_terms = dense_terms.reshape((panel_list + 1) * ncol, half, lanes)
    oz = jnp.arange(nz)[:, None, None]
    ox = jnp.arange(nx)[None, :, None]
    oj = jnp.arange(slot_dev)[None, None, :]
    rs_order = (((oz * nx + ox) * nc + my_core) * slot_dev + oj).reshape(-1)
    slot_match = slot_lookup[None, :] == rs_order[:, None]
    pos_panel = jnp.arange(store_slots, dtype=jnp.int32) // most_kept
    pos_index = pos_panel * ncol + column_list.reshape(-1)
    pos_kept = kept_grid.reshape(-1)
    term_index = jnp.sum(jnp.where(slot_match, pos_index[None, :], 0), axis=1)
    term_kept = jnp.any(slot_match & pos_kept[None, :], axis=1)
    terms = dense_terms[jnp.where(term_kept, term_index, panel_list * ncol)]
    terms, gathered = lax.optimization_barrier((terms, gathered))
    gathered = jnp.concatenate([gathered, sibling(gathered)], axis=0)
    weight_grad = lax.psum_scatter(terms, "z", scatter_dimension=0, tiled=True)
    x_blocks = weight_grad.reshape(nx, slot_dev, half, lanes)
    weight_grad = jnp.sum(lax.all_to_all(x_blocks, "x", 0, 0), axis=0)
    weight_grad = (weight_grad * grad_scale).reshape(slot_dev, blk * blk)

    dense_w = jnp.where(
        has_tile.reshape(-1)[:, None, None], gathered[dense_rows], jnp.zeros((), gathered.dtype)
    ).reshape(panel_list, ncol, half, lanes)
    normed_grad = jnp.einsum("cthl,pcrl->tprh", expand, dense_w, preferred_element_type=jnp.float32)
    normed_grad = normed_grad.reshape(tok_rows, width)

    scaled = gain_row[None, :] * normed_grad
    inner = jnp.sum(scaled * inputs_f, axis=1, keepdims=True) / width
    input_grad = (recip * scaled - inputs_f * recip**3 * inner).astype(jnp.bfloat16)
    handed = shifted(input_grad, "section", -1)
    return (handed[None], weight_grad[None])


def solution(mesh):
    sec, fs = mesh.devices.shape
    mesh = jax.sharding.Mesh(mesh.devices.reshape(sec, fs // 8, 4, 2), ("section",) + FS)
    placed = (
        P("section", FS, None),
        P("section", FS, None),
        P("section", None),
        P("section", FS, None),
        P("section", None, None),
        P("section", None),
        P("section", None),
    )
    return jax.shard_map(
        local,
        mesh=mesh,
        in_specs=placed,
        out_specs=(P("section", FS, None), P("section", FS, None)),
        check_vma=False,
    )
```

```python
import jax
import jax.numpy as jnp
from jax import lax
from jax.sharding import PartitionSpec as P

EPS = 1e-05
FS = ("z", "x", "core")


def shifted(value, axis, steps):
    count = lax.axis_size(axis)
    leading, last = (max(0, -steps), min(count, count - steps))
    return lax.ppermute(value, axis, [(source, source + steps) for source in range(leading, last)])


def sibling(value):
    count = lax.axis_size("core")
    return lax.ppermute(value, "core", [(source, (source + 1) % count) for source in range(count)])


def local(acts, out_grad, norm_gain, tiles, tile_cols, tile_count, tile_store_slot):
    inputs_f = acts[0].astype(jnp.float32)
    key_grad = out_grad[0]
    gain_row = norm_gain[0]
    column_list = tile_cols[0]
    count_list = tile_count[0]
    slot_lookup = tile_store_slot[0]
    tok_rows, width = inputs_f.shape
    kv_width = key_grad.shape[1]
    panel_list, most_kept = column_list.shape
    blk = width // panel_list
    ncol = kv_width // blk
    store_slots = panel_list * most_kept
    slot_dev = tiles.shape[1]
    nz, nx, nc = (lax.axis_size(a) for a in FS)
    half = blk // 2
    lanes = 2 * blk
    grad_scale = (tok_rows * nz * nx * nc) ** (-0.5)

    own_tiles = tiles[0].reshape(slot_dev, half, lanes)
    gathered = jnp.concatenate(
        [own_tiles]
        + [lax.ppermute(own_tiles, "x", [(src, (src + s) % nx) for src in range(nx)]) for s in range(1, nx)],
        axis=0,
    )
    gathered = lax.all_gather(gathered, "z", axis=0, tiled=True)
    slot_ids = jnp.arange(store_slots, dtype=jnp.int32)

    my_core = lax.axis_index("core")
    my_x = lax.axis_index("x")

    def row_of(slot):
        holder = slot // slot_dev
        half_of = (holder % nc - my_core) % nc
        chip = holder // nc
        shift = (my_x - chip % nx) % nx
        return half_of * (nz * nx * slot_dev) + ((chip // nx) * nx + shift) * slot_dev + slot % slot_dev

    kept_grid = jnp.arange(most_kept)[None, :] < count_list[:, None]
    col_hit = (column_list[:, :, None] == jnp.arange(ncol)[None, None, :]) & kept_grid[:, :, None]
    has_tile = jnp.any(col_hit, axis=1)
    hit_rows = jnp.sum(jnp.where(col_hit, row_of(slot_lookup.reshape(panel_list, most_kept))[:, :, None], 0), axis=1)
    dense_rows = hit_rows.reshape(-1)

    mean_sq = jnp.mean(inputs_f * inputs_f, axis=1, keepdims=True)
    recip = lax.rsqrt(mean_sq + EPS)
    normed = (inputs_f * recip * gain_row[None, :]).astype(jnp.bfloat16)
    pair_tokens = nc * tok_rows
    normed_pair = jnp.concatenate([normed, sibling(normed)], axis=0)
    og_pair = jnp.concatenate([key_grad, sibling(key_grad)], axis=0)

    og_blocks = key_grad.reshape(tok_rows, ncol, blk).transpose(1, 0, 2)
    diag = (jnp.arange(2)[:, None] == jnp.arange(lanes)[None, :] // blk)
    og_wide = jnp.concatenate([og_blocks, og_blocks], axis=2)
    expand = jnp.where(diag[None, None, :, :], og_wide[:, :, None, :], jnp.zeros((), key_grad.dtype))

    pair_blocks = og_pair.reshape(pair_tokens, ncol, blk).transpose(1, 0, 2)
    pair_wide = jnp.concatenate([pair_blocks, pair_blocks], axis=2)
    expand_pair = jnp.where(diag[None, None, :, :], pair_wide[:, :, None, :], jnp.zeros((), key_grad.dtype))
    normed_pairs = normed_pair.reshape(pair_tokens, panel_list, half, 2).transpose(1, 2, 3, 0)
    normed_pairs = normed_pairs.reshape(panel_list, half, 2 * pair_tokens)
    expand_k = expand_pair.transpose(0, 2, 1, 3).reshape(ncol, 2 * pair_tokens, lanes)
    normed_pairs = jnp.concatenate([normed_pairs, jnp.zeros((1, half, 2 * pair_tokens), normed_pairs.dtype)], axis=0)
    dense_terms = jnp.dot(
        normed_pairs.reshape((panel_list + 1) * half, 2 * pair_tokens),
        expand_k.transpose(1, 0, 2).reshape(2 * pair_tokens, ncol * lanes),
        preferred_element_type=jnp.float32,
    )
    dense_terms = dense_terms.reshape(panel_list + 1, half, ncol, lanes).transpose(0, 2, 1, 3)
    dense_terms = dense_terms.reshape((panel_list + 1) * ncol, half, lanes)
    oz = jnp.arange(nz)[:, None, None]
    ox = jnp.arange(nx)[None, :, None]
    oj = jnp.arange(slot_dev)[None, None, :]
    rs_order = (((oz * nx + (ox + my_x) % nx) * nc + my_core) * slot_dev + oj).reshape(-1)
    slot_match = slot_lookup[None, :] == rs_order[:, None]
    pos_panel = jnp.arange(store_slots, dtype=jnp.int32) // most_kept
    pos_index = pos_panel * ncol + column_list.reshape(-1)
    pos_kept = kept_grid.reshape(-1)
    term_index = jnp.sum(jnp.where(slot_match, pos_index[None, :], 0), axis=1)
    term_kept = jnp.any(slot_match & pos_kept[None, :], axis=1)
    terms = dense_terms[jnp.where(term_kept, term_index, panel_list * ncol)] * grad_scale
    terms, gathered = lax.optimization_barrier((terms, gathered))
    gathered = jnp.concatenate([gathered, sibling(gathered)], axis=0)
    weight_grad = lax.psum_scatter(terms, "z", scatter_dimension=0, tiled=True)
    x_blocks = weight_grad.reshape(nx, slot_dev, half, lanes)
    own_sum = x_blocks[0]
    for s in range(1, nx):
        own_sum = own_sum + lax.ppermute(x_blocks[s], "x", [(src, (src + s) % nx) for src in range(nx)])
    weight_grad = own_sum.reshape(slot_dev, blk * blk)

    dense_w = jnp.where(
        has_tile.reshape(-1)[:, None, None], gathered[dense_rows], jnp.zeros((), gathered.dtype)
    ).reshape(panel_list, ncol, half, lanes)
    normed_grad = jnp.einsum("cthl,pcrl->tprh", expand, dense_w, preferred_element_type=jnp.float32)
    normed_grad = normed_grad.reshape(tok_rows, width)

    scaled = gain_row[None, :] * normed_grad
    inner = jnp.sum(scaled * inputs_f, axis=1, keepdims=True) / width
    input_grad = (recip * scaled - inputs_f * recip**3 * inner).astype(jnp.bfloat16)
    handed = shifted(input_grad, "section", -1)
    return (handed[None], weight_grad[None])


def solution(mesh):
    sec, fs = mesh.devices.shape
    mesh = jax.sharding.Mesh(mesh.devices.reshape(sec, fs // 8, 4, 2), ("section",) + FS)
    placed = (
        P("section", FS, None),
        P("section", FS, None),
        P("section", None),
        P("section", FS, None),
        P("section", None, None),
        P("section", None),
        P("section", None),
    )
    return jax.shard_map(
        local,
        mesh=mesh,
        in_specs=placed,
        out_specs=(P("section", FS, None), P("section", FS, None)),
        check_vma=False,
    )
```

```python
import jax
import jax.numpy as jnp
from jax import lax
from jax.sharding import PartitionSpec as P

EPS = 1e-05
FS = ("z", "x", "core")


def shifted(value, axis, steps):
    count = lax.axis_size(axis)
    leading, last = (max(0, -steps), min(count, count - steps))
    return lax.ppermute(value, axis, [(source, source + steps) for source in range(leading, last)])


def sibling(value):
    count = lax.axis_size("core")
    return lax.ppermute(value, "core", [(source, (source + 1) % count) for source in range(count)])


def local(acts, out_grad, norm_gain, tiles, tile_cols, tile_count, tile_store_slot):
    inputs_f = acts[0].astype(jnp.float32)
    key_grad = out_grad[0]
    gain_row = norm_gain[0]
    column_list = tile_cols[0]
    count_list = tile_count[0]
    slot_lookup = tile_store_slot[0]
    tok_rows, width = inputs_f.shape
    kv_width = key_grad.shape[1]
    panel_list, most_kept = column_list.shape
    blk = width // panel_list
    ncol = kv_width // blk
    store_slots = panel_list * most_kept
    slot_dev = tiles.shape[1]
    nz, nx, nc = (lax.axis_size(a) for a in FS)
    half = blk // 2
    lanes = 2 * blk
    grad_scale = (tok_rows * nz * nx * nc) ** (-0.5)

    own_tiles = tiles[0].reshape(slot_dev, half, lanes)
    copies = jnp.broadcast_to(own_tiles[None], (nx,) + own_tiles.shape)
    gathered = lax.all_to_all(copies, "x", 0, 0).reshape(nx * slot_dev, half, lanes)
    gathered = lax.all_gather(gathered, "z", axis=0, tiled=True)
    slot_ids = jnp.arange(store_slots, dtype=jnp.int32)

    my_core = lax.axis_index("core")
    my_x = lax.axis_index("x")

    def row_of(slot):
        holder = slot // slot_dev
        half_of = (holder % nc - my_core) % nc
        chip = holder // nc
        shift = chip % nx
        return half_of * (nz * nx * slot_dev) + ((chip // nx) * nx + shift) * slot_dev + slot % slot_dev

    kept_grid = jnp.arange(most_kept)[None, :] < count_list[:, None]
    col_hit = (column_list[:, :, None] == jnp.arange(ncol)[None, None, :]) & kept_grid[:, :, None]
    has_tile = jnp.any(col_hit, axis=1)
    hit_rows = jnp.sum(jnp.where(col_hit, row_of(slot_lookup.reshape(panel_list, most_kept))[:, :, None], 0), axis=1)
    dense_rows = hit_rows.reshape(-1)

    mean_sq = jnp.mean(inputs_f * inputs_f, axis=1, keepdims=True)
    recip = lax.rsqrt(mean_sq + EPS)
    normed = (inputs_f * recip * gain_row[None, :]).astype(jnp.bfloat16)
    pair_tokens = nc * tok_rows
    normed_pair = jnp.concatenate([normed, sibling(normed)], axis=0)
    og_pair = jnp.concatenate([key_grad, sibling(key_grad)], axis=0)

    og_blocks = key_grad.reshape(tok_rows, ncol, blk).transpose(1, 0, 2)
    diag = (jnp.arange(2)[:, None] == jnp.arange(lanes)[None, :] // blk)
    og_wide = jnp.concatenate([og_blocks, og_blocks], axis=2)
    expand = jnp.where(diag[None, None, :, :], og_wide[:, :, None, :], jnp.zeros((), key_grad.dtype))

    pair_blocks = og_pair.reshape(pair_tokens, ncol, blk).transpose(1, 0, 2)
    pair_wide = jnp.concatenate([pair_blocks, pair_blocks], axis=2)
    expand_pair = jnp.where(diag[None, None, :, :], pair_wide[:, :, None, :], jnp.zeros((), key_grad.dtype))
    normed_pairs = normed_pair.reshape(pair_tokens, panel_list, half, 2).transpose(1, 2, 3, 0)
    normed_pairs = normed_pairs.reshape(panel_list, half, 2 * pair_tokens)
    expand_k = expand_pair.transpose(0, 2, 1, 3).reshape(ncol, 2 * pair_tokens, lanes)
    normed_pairs = jnp.concatenate([normed_pairs, jnp.zeros((1, half, 2 * pair_tokens), normed_pairs.dtype)], axis=0)
    dense_terms = jnp.dot(
        normed_pairs.reshape((panel_list + 1) * half, 2 * pair_tokens),
        expand_k.transpose(1, 0, 2).reshape(2 * pair_tokens, ncol * lanes),
        preferred_element_type=jnp.float32,
    )
    dense_terms = dense_terms.reshape(panel_list + 1, half, ncol, lanes).transpose(0, 2, 1, 3)
    dense_terms = dense_terms.reshape((panel_list + 1) * ncol, half, lanes)
    oz = jnp.arange(nz)[:, None, None]
    ox = jnp.arange(nx)[None, :, None]
    oj = jnp.arange(slot_dev)[None, None, :]
    rs_order = (((oz * nx + ox) * nc + my_core) * slot_dev + oj).reshape(-1)
    slot_match = slot_lookup[None, :] == rs_order[:, None]
    pos_panel = jnp.arange(store_slots, dtype=jnp.int32) // most_kept
    pos_index = pos_panel * ncol + column_list.reshape(-1)
    pos_kept = kept_grid.reshape(-1)
    term_index = jnp.sum(jnp.where(slot_match, pos_index[None, :], 0), axis=1)
    term_kept = jnp.any(slot_match & pos_kept[None, :], axis=1)
    terms = dense_terms[jnp.where(term_kept, term_index, panel_list * ncol)]
    terms, gathered = lax.optimization_barrier((terms, gathered))
    gathered = jnp.concatenate([gathered, sibling(gathered)], axis=0)
    weight_grad = lax.psum_scatter(terms, "z", scatter_dimension=0, tiled=True)
    x_blocks = weight_grad.reshape(nx, slot_dev, half, lanes)
    own_sum = lax.dynamic_index_in_dim(x_blocks, my_x, axis=0, keepdims=False)
    for s in range(1, nx):
        outgoing = lax.dynamic_index_in_dim(x_blocks, (my_x + s) % nx, axis=0, keepdims=False)
        own_sum = own_sum + lax.ppermute(outgoing, "x", [(src, (src + s) % nx) for src in range(nx)])
    weight_grad = own_sum
    weight_grad = (weight_grad * grad_scale).reshape(slot_dev, blk * blk)

    dense_w = jnp.where(
        has_tile.reshape(-1)[:, None, None], gathered[dense_rows], jnp.zeros((), gathered.dtype)
    ).reshape(panel_list, ncol, half, lanes)
    normed_grad = jnp.einsum("cthl,pcrl->tprh", expand, dense_w, preferred_element_type=jnp.float32)
    normed_grad = normed_grad.reshape(tok_rows, width)

    scaled = gain_row[None, :] * normed_grad
    inner = jnp.sum(scaled * inputs_f, axis=1, keepdims=True) / width
    input_grad = (recip * scaled - inputs_f * recip**3 * inner).astype(jnp.bfloat16)
    handed = shifted(input_grad, "section", -1)
    return (handed[None], weight_grad[None])


def solution(mesh):
    sec, fs = mesh.devices.shape
    mesh = jax.sharding.Mesh(mesh.devices.reshape(sec, fs // 8, 4, 2), ("section",) + FS)
    placed = (
        P("section", FS, None),
        P("section", FS, None),
        P("section", None),
        P("section", FS, None),
        P("section", None, None),
        P("section", None),
        P("section", None),
    )
    return jax.shard_map(
        local,
        mesh=mesh,
        in_specs=placed,
        out_specs=(P("section", FS, None), P("section", FS, None)),
        check_vma=False,
    )
```

```python
import jax
import jax.numpy as jnp
from jax import lax
from jax.sharding import PartitionSpec as P

EPS = 1e-05
FS = ("z", "x", "core")


def shifted(value, axis, steps):
    count = lax.axis_size(axis)
    leading, last = (max(0, -steps), min(count, count - steps))
    return lax.ppermute(value, axis, [(source, source + steps) for source in range(leading, last)])


def sibling(value):
    count = lax.axis_size("core")
    return lax.ppermute(value, "core", [(source, (source + 1) % count) for source in range(count)])


def local(acts, out_grad, norm_gain, tiles, tile_cols, tile_count, tile_store_slot):
    inputs_f = acts[0].astype(jnp.float32)
    key_grad = out_grad[0]
    gain_row = norm_gain[0]
    column_list = tile_cols[0]
    count_list = tile_count[0]
    slot_lookup = tile_store_slot[0]
    tok_rows, width = inputs_f.shape
    kv_width = key_grad.shape[1]
    panel_list, most_kept = column_list.shape
    blk = width // panel_list
    ncol = kv_width // blk
    store_slots = panel_list * most_kept
    slot_dev = tiles.shape[1]
    nz, nx, nc = (lax.axis_size(a) for a in FS)
    half = blk // 2
    lanes = 2 * blk
    grad_scale = (tok_rows * nz * nx * nc) ** (-0.5)

    own_tiles = tiles[0].reshape(slot_dev, half, lanes)
    shift_order = sorted(range(1, nx), key=lambda s: -min(s, nx - s))
    moved = {s: lax.ppermute(own_tiles, "x", [(src, (src + s) % nx) for src in range(nx)]) for s in shift_order}
    gathered = jnp.concatenate([own_tiles] + [moved[s] for s in range(1, nx)], axis=0)
    gathered = lax.all_gather(gathered, "z", axis=0, tiled=True)
    slot_ids = jnp.arange(store_slots, dtype=jnp.int32)

    my_core = lax.axis_index("core")
    my_x = lax.axis_index("x")

    def row_of(slot):
        holder = slot // slot_dev
        half_of = (holder % nc - my_core) % nc
        chip = holder // nc
        shift = (my_x - chip % nx) % nx
        return half_of * (nz * nx * slot_dev) + ((chip // nx) * nx + shift) * slot_dev + slot % slot_dev

    kept_grid = jnp.arange(most_kept)[None, :] < count_list[:, None]
    col_hit = (column_list[:, :, None] == jnp.arange(ncol)[None, None, :]) & kept_grid[:, :, None]
    has_tile = jnp.any(col_hit, axis=1)
    hit_rows = jnp.sum(jnp.where(col_hit, row_of(slot_lookup.reshape(panel_list, most_kept))[:, :, None], 0), axis=1)
    dense_rows = hit_rows.reshape(-1)

    mean_sq = jnp.mean(inputs_f * inputs_f, axis=1, keepdims=True)
    recip = lax.rsqrt(mean_sq + EPS)
    normed = (inputs_f * recip * gain_row[None, :]).astype(jnp.bfloat16)
    pair_tokens = nc * tok_rows
    normed_pair = jnp.concatenate([normed, sibling(normed)], axis=0)
    og_pair = jnp.concatenate([key_grad, sibling(key_grad)], axis=0)

    og_blocks = key_grad.reshape(tok_rows, ncol, blk).transpose(1, 0, 2)
    diag = (jnp.arange(2)[:, None] == jnp.arange(lanes)[None, :] // blk)
    og_wide = jnp.concatenate([og_blocks, og_blocks], axis=2)
    expand = jnp.where(diag[None, None, :, :], og_wide[:, :, None, :], jnp.zeros((), key_grad.dtype))

    pair_blocks = og_pair.reshape(pair_tokens, ncol, blk).transpose(1, 0, 2)
    pair_wide = jnp.concatenate([pair_blocks, pair_blocks], axis=2)
    expand_pair = jnp.where(diag[None, None, :, :], pair_wide[:, :, None, :], jnp.zeros((), key_grad.dtype))
    normed_pairs = normed_pair.reshape(pair_tokens, panel_list, half, 2).transpose(1, 2, 3, 0)
    normed_pairs = normed_pairs.reshape(panel_list, half, 2 * pair_tokens)
    expand_k = expand_pair.transpose(0, 2, 1, 3).reshape(ncol, 2 * pair_tokens, lanes)
    normed_pairs = jnp.concatenate([normed_pairs, jnp.zeros((1, half, 2 * pair_tokens), normed_pairs.dtype)], axis=0)
    dense_terms = jnp.dot(
        normed_pairs.reshape((panel_list + 1) * half, 2 * pair_tokens),
        expand_k.transpose(1, 0, 2).reshape(2 * pair_tokens, ncol * lanes),
        preferred_element_type=jnp.float32,
    )
    dense_terms = dense_terms.reshape(panel_list + 1, half, ncol, lanes).transpose(0, 2, 1, 3)
    dense_terms = dense_terms.reshape((panel_list + 1) * ncol, half, lanes)
    oz = jnp.arange(nz)[:, None, None]
    ox = jnp.arange(nx)[None, :, None]
    oj = jnp.arange(slot_dev)[None, None, :]
    rs_order = (((oz * nx + ox) * nc + my_core) * slot_dev + oj).reshape(-1)
    slot_match = slot_lookup[None, :] == rs_order[:, None]
    pos_panel = jnp.arange(store_slots, dtype=jnp.int32) // most_kept
    pos_index = pos_panel * ncol + column_list.reshape(-1)
    pos_kept = kept_grid.reshape(-1)
    term_index = jnp.sum(jnp.where(slot_match, pos_index[None, :], 0), axis=1)
    term_kept = jnp.any(slot_match & pos_kept[None, :], axis=1)
    terms = dense_terms[jnp.where(term_kept, term_index, panel_list * ncol)]
    terms, gathered = lax.optimization_barrier((terms, gathered))
    gathered = jnp.concatenate([gathered, sibling(gathered)], axis=0)
    weight_grad = lax.psum_scatter(terms, "z", scatter_dimension=0, tiled=True)
    x_blocks = weight_grad.reshape(nx, slot_dev, half, lanes)
    own_sum = lax.dynamic_index_in_dim(x_blocks, my_x, axis=0, keepdims=False)
    for s in shift_order:
        outgoing = lax.dynamic_index_in_dim(x_blocks, (my_x + s) % nx, axis=0, keepdims=False)
        own_sum = own_sum + lax.ppermute(outgoing, "x", [(src, (src + s) % nx) for src in range(nx)])
    weight_grad = own_sum
    weight_grad = (weight_grad * grad_scale).reshape(slot_dev, blk * blk)

    dense_w = jnp.where(
        has_tile.reshape(-1)[:, None, None], gathered[dense_rows], jnp.zeros((), gathered.dtype)
    ).reshape(panel_list, ncol, half, lanes)
    normed_grad = jnp.einsum("cthl,pcrl->tprh", expand, dense_w, preferred_element_type=jnp.float32)
    normed_grad = normed_grad.reshape(tok_rows, width)

    scaled = gain_row[None, :] * normed_grad
    inner = jnp.sum(scaled * inputs_f, axis=1, keepdims=True) / width
    input_grad = (recip * scaled - inputs_f * recip**3 * inner).astype(jnp.bfloat16)
    handed = shifted(input_grad, "section", -1)
    return (handed[None], weight_grad[None])


def solution(mesh):
    sec, fs = mesh.devices.shape
    mesh = jax.sharding.Mesh(mesh.devices.reshape(sec, fs // 8, 4, 2), ("section",) + FS)
    placed = (
        P("section", FS, None),
        P("section", FS, None),
        P("section", None),
        P("section", FS, None),
        P("section", None, None),
        P("section", None),
        P("section", None),
    )
    return jax.shard_map(
        local,
        mesh=mesh,
        in_specs=placed,
        out_specs=(P("section", FS, None), P("section", FS, None)),
        check_vma=False,
    )
```

```python
import jax
import jax.numpy as jnp
from jax import lax
from jax.sharding import PartitionSpec as P

EPS = 1e-05
FS = ("z", "x", "core")


def shifted(value, axis, steps):
    count = lax.axis_size(axis)
    leading, last = (max(0, -steps), min(count, count - steps))
    return lax.ppermute(value, axis, [(source, source + steps) for source in range(leading, last)])


def sibling(value):
    count = lax.axis_size("core")
    return lax.ppermute(value, "core", [(source, (source + 1) % count) for source in range(count)])


def local(acts, out_grad, norm_gain, tiles, tile_cols, tile_count, tile_store_slot):
    inputs_f = acts[0].astype(jnp.float32)
    key_grad = out_grad[0]
    gain_row = norm_gain[0]
    column_list = tile_cols[0]
    count_list = tile_count[0]
    slot_lookup = tile_store_slot[0]
    tok_rows, width = inputs_f.shape
    kv_width = key_grad.shape[1]
    panel_list, most_kept = column_list.shape
    blk = width // panel_list
    ncol = kv_width // blk
    store_slots = panel_list * most_kept
    slot_dev = tiles.shape[1]
    nz, nx, nc = (lax.axis_size(a) for a in FS)
    half = blk // 2
    lanes = 2 * blk
    grad_scale = (tok_rows * nz * nx * nc) ** (-0.5)

    own_tiles = tiles[0].reshape(slot_dev, half, lanes)
    shift_order = sorted(range(1, nx), key=lambda s: -min(s, nx - s))
    moved = {s: lax.ppermute(own_tiles, "x", [(src, (src + s) % nx) for src in range(nx)]) for s in shift_order}
    gathered = jnp.concatenate([own_tiles] + [moved[s] for s in range(1, nx)], axis=0)
    gathered = lax.all_gather(gathered, "z", axis=0, tiled=True)
    slot_ids = jnp.arange(store_slots, dtype=jnp.int32)

    my_core = lax.axis_index("core")
    my_x = lax.axis_index("x")

    def row_of(slot):
        holder = slot // slot_dev
        half_of = (holder % nc - my_core) % nc
        chip = holder // nc
        shift = (my_x - chip % nx) % nx
        return half_of * (nz * nx * slot_dev) + ((chip // nx) * nx + shift) * slot_dev + slot % slot_dev

    kept_grid = jnp.arange(most_kept)[None, :] < count_list[:, None]
    col_hit = (column_list[:, :, None] == jnp.arange(ncol)[None, None, :]) & kept_grid[:, :, None]
    has_tile = jnp.any(col_hit, axis=1)
    hit_rows = jnp.sum(jnp.where(col_hit, row_of(slot_lookup.reshape(panel_list, most_kept))[:, :, None], 0), axis=1)
    dense_rows = hit_rows.reshape(-1)

    mean_sq = jnp.mean(inputs_f * inputs_f, axis=1, keepdims=True)
    recip = lax.rsqrt(mean_sq + EPS)
    normed = (inputs_f * recip * gain_row[None, :]).astype(jnp.bfloat16)
    pair_tokens = nc * tok_rows
    both = sibling(jnp.concatenate([normed, key_grad], axis=1))
    normed_pair = jnp.concatenate([normed, both[:, :width]], axis=0)
    og_pair = jnp.concatenate([key_grad, both[:, width:]], axis=0)

    og_blocks = key_grad.reshape(tok_rows, ncol, blk).transpose(1, 0, 2)
    diag = (jnp.arange(2)[:, None] == jnp.arange(lanes)[None, :] // blk)
    og_wide = jnp.concatenate([og_blocks, og_blocks], axis=2)
    expand = jnp.where(diag[None, None, :, :], og_wide[:, :, None, :], jnp.zeros((), key_grad.dtype))

    pair_blocks = og_pair.reshape(pair_tokens, ncol, blk).transpose(1, 0, 2)
    pair_wide = jnp.concatenate([pair_blocks, pair_blocks], axis=2)
    expand_pair = jnp.where(diag[None, None, :, :], pair_wide[:, :, None, :], jnp.zeros((), key_grad.dtype))
    normed_pairs = normed_pair.reshape(pair_tokens, panel_list, half, 2).transpose(1, 2, 3, 0)
    normed_pairs = normed_pairs.reshape(panel_list, half, 2 * pair_tokens)
    expand_k = expand_pair.transpose(0, 2, 1, 3).reshape(ncol, 2 * pair_tokens, lanes)
    normed_pairs = jnp.concatenate([normed_pairs, jnp.zeros((1, half, 2 * pair_tokens), normed_pairs.dtype)], axis=0)
    dense_terms = jnp.dot(
        normed_pairs.reshape((panel_list + 1) * half, 2 * pair_tokens),
        expand_k.transpose(1, 0, 2).reshape(2 * pair_tokens, ncol * lanes),
        preferred_element_type=jnp.float32,
    )
    dense_terms = dense_terms.reshape(panel_list + 1, half, ncol, lanes).transpose(0, 2, 1, 3)
    dense_terms = dense_terms.reshape((panel_list + 1) * ncol, half, lanes)
    oz = jnp.arange(nz)[:, None, None]
    ox = jnp.arange(nx)[None, :, None]
    oj = jnp.arange(slot_dev)[None, None, :]
    rs_order = (((oz * nx + ox) * nc + my_core) * slot_dev + oj).reshape(-1)
    slot_match = slot_lookup[None, :] == rs_order[:, None]
    pos_panel = jnp.arange(store_slots, dtype=jnp.int32) // most_kept
    pos_index = pos_panel * ncol + column_list.reshape(-1)
    pos_kept = kept_grid.reshape(-1)
    term_index = jnp.sum(jnp.where(slot_match, pos_index[None, :], 0), axis=1)
    term_kept = jnp.any(slot_match & pos_kept[None, :], axis=1)
    terms = dense_terms[jnp.where(term_kept, term_index, panel_list * ncol)]
    terms, gathered = lax.optimization_barrier((terms, gathered))
    gathered = jnp.concatenate([gathered, sibling(gathered)], axis=0)
    weight_grad = lax.psum_scatter(terms, "z", scatter_dimension=0, tiled=True)
    x_blocks = weight_grad.reshape(nx, slot_dev, half, lanes)
    own_sum = lax.dynamic_index_in_dim(x_blocks, my_x, axis=0, keepdims=False)
    for s in shift_order:
        outgoing = lax.dynamic_index_in_dim(x_blocks, (my_x + s) % nx, axis=0, keepdims=False)
        own_sum = own_sum + lax.ppermute(outgoing, "x", [(src, (src + s) % nx) for src in range(nx)])
    weight_grad = own_sum
    weight_grad = (weight_grad * grad_scale).reshape(slot_dev, blk * blk)

    dense_w = jnp.where(
        has_tile.reshape(-1)[:, None, None], gathered[dense_rows], jnp.zeros((), gathered.dtype)
    ).reshape(panel_list, ncol, half, lanes)
    normed_grad = jnp.einsum("cthl,pcrl->tprh", expand, dense_w, preferred_element_type=jnp.float32)
    normed_grad = normed_grad.reshape(tok_rows, width)

    scaled = gain_row[None, :] * normed_grad
    inner = jnp.sum(scaled * inputs_f, axis=1, keepdims=True) / width
    input_grad = (recip * scaled - inputs_f * recip**3 * inner).astype(jnp.bfloat16)
    handed = shifted(input_grad, "section", -1)
    return (handed[None], weight_grad[None])


def solution(mesh):
    sec, fs = mesh.devices.shape
    mesh = jax.sharding.Mesh(mesh.devices.reshape(sec, fs // 8, 4, 2), ("section",) + FS)
    placed = (
        P("section", FS, None),
        P("section", FS, None),
        P("section", None),
        P("section", FS, None),
        P("section", None, None),
        P("section", None),
        P("section", None),
    )
    return jax.shard_map(
        local,
        mesh=mesh,
        in_specs=placed,
        out_specs=(P("section", FS, None), P("section", FS, None)),
        check_vma=False,
    )
```

```python
import jax
import jax.numpy as jnp
from jax import lax
from jax.sharding import PartitionSpec as P

EPS = 1e-05
FS = ("z", "x", "core")


def shifted(value, axis, steps):
    count = lax.axis_size(axis)
    leading, last = (max(0, -steps), min(count, count - steps))
    return lax.ppermute(value, axis, [(source, source + steps) for source in range(leading, last)])


def sibling(value):
    count = lax.axis_size("core")
    return lax.ppermute(value, "core", [(source, (source + 1) % count) for source in range(count)])


def local(acts, out_grad, norm_gain, tiles, tile_cols, tile_count, tile_store_slot):
    inputs_f = acts[0].astype(jnp.float32)
    key_grad = out_grad[0]
    gain_row = norm_gain[0]
    column_list = tile_cols[0]
    count_list = tile_count[0]
    slot_lookup = tile_store_slot[0]
    tok_rows, width = inputs_f.shape
    kv_width = key_grad.shape[1]
    panel_list, most_kept = column_list.shape
    blk = width // panel_list
    ncol = kv_width // blk
    store_slots = panel_list * most_kept
    slot_dev = tiles.shape[1]
    nz, nx, nc = (lax.axis_size(a) for a in FS)
    half = blk // 2
    lanes = 2 * blk
    grad_scale = (tok_rows * nz * nx * nc) ** (-0.5)

    own_tiles = tiles[0].reshape(slot_dev, half, lanes)
    shift_order = sorted(range(1, nx), key=lambda s: -min(s, nx - s))
    moved = {s: lax.ppermute(own_tiles, "x", [(src, (src + s) % nx) for src in range(nx)]) for s in shift_order}
    gathered = jnp.concatenate([own_tiles] + [moved[s] for s in range(1, nx)], axis=0)
    gathered = lax.all_gather(gathered, "z", axis=0, tiled=True)
    slot_ids = jnp.arange(store_slots, dtype=jnp.int32)

    my_core = lax.axis_index("core")
    my_x = lax.axis_index("x")

    def row_of(slot):
        holder = slot // slot_dev
        half_of = (holder % nc - my_core) % nc
        chip = holder // nc
        shift = (my_x - chip % nx) % nx
        return half_of * (nz * nx * slot_dev) + ((chip // nx) * nx + shift) * slot_dev + slot % slot_dev

    kept_grid = jnp.arange(most_kept)[None, :] < count_list[:, None]
    col_hit = (column_list[:, :, None] == jnp.arange(ncol)[None, None, :]) & kept_grid[:, :, None]
    has_tile = jnp.any(col_hit, axis=1)
    hit_rows = jnp.sum(jnp.where(col_hit, row_of(slot_lookup.reshape(panel_list, most_kept))[:, :, None], 0), axis=1)
    dense_rows = hit_rows.reshape(-1)

    mean_sq = jnp.mean(inputs_f * inputs_f, axis=1, keepdims=True)
    recip = lax.rsqrt(mean_sq + EPS)
    normed = (inputs_f * recip * gain_row[None, :]).astype(jnp.bfloat16)
    pair_tokens = nc * tok_rows
    both = sibling(jnp.concatenate([normed, key_grad], axis=1))
    normed_pair = jnp.concatenate([normed, both[:, :width]], axis=0)
    og_pair = jnp.concatenate([key_grad, both[:, width:]], axis=0)

    og_blocks = key_grad.reshape(tok_rows, ncol, blk).transpose(1, 0, 2)
    diag = (jnp.arange(2)[:, None] == jnp.arange(lanes)[None, :] // blk)
    og_wide = jnp.concatenate([og_blocks, og_blocks], axis=2)
    expand = jnp.where(diag[None, None, :, :], og_wide[:, :, None, :], jnp.zeros((), key_grad.dtype))

    pair_blocks = og_pair.reshape(pair_tokens, ncol, blk).transpose(1, 0, 2)
    pair_wide = jnp.concatenate([pair_blocks, pair_blocks], axis=2)
    expand_pair = jnp.where(diag[None, None, :, :], pair_wide[:, :, None, :], jnp.zeros((), key_grad.dtype))
    normed_pairs = normed_pair.reshape(pair_tokens, panel_list, half, 2).transpose(1, 2, 3, 0)
    normed_pairs = normed_pairs.reshape(panel_list, half, 2 * pair_tokens)
    expand_k = expand_pair.transpose(0, 2, 1, 3).reshape(ncol, 2 * pair_tokens, lanes)
    normed_pairs = jnp.concatenate([normed_pairs, jnp.zeros((1, half, 2 * pair_tokens), normed_pairs.dtype)], axis=0)
    dense_terms = jnp.dot(
        normed_pairs.reshape((panel_list + 1) * half, 2 * pair_tokens),
        expand_k.transpose(1, 0, 2).reshape(2 * pair_tokens, ncol * lanes),
        preferred_element_type=jnp.float32,
    )
    dense_terms = dense_terms.reshape(panel_list + 1, half, ncol, lanes).transpose(0, 2, 1, 3)
    dense_terms = dense_terms.reshape((panel_list + 1) * ncol, half, lanes)
    oz = jnp.arange(nz)[:, None, None]
    ox = jnp.arange(nx)[None, :, None]
    oj = jnp.arange(slot_dev)[None, None, :]
    rs_order = (((oz * nx + (ox + my_x) % nx) * nc + my_core) * slot_dev + oj).reshape(-1)
    slot_match = slot_lookup[None, :] == rs_order[:, None]
    pos_panel = jnp.arange(store_slots, dtype=jnp.int32) // most_kept
    pos_index = pos_panel * ncol + column_list.reshape(-1)
    pos_kept = kept_grid.reshape(-1)
    term_index = jnp.sum(jnp.where(slot_match, pos_index[None, :], 0), axis=1)
    term_kept = jnp.any(slot_match & pos_kept[None, :], axis=1)
    terms = dense_terms[jnp.where(term_kept, term_index, panel_list * ncol)] * grad_scale
    terms, gathered = lax.optimization_barrier((terms, gathered))
    gathered = jnp.concatenate([gathered, sibling(gathered)], axis=0)
    weight_grad = lax.psum_scatter(terms, "z", scatter_dimension=0, tiled=True)
    x_blocks = weight_grad.reshape(nx, slot_dev, half, lanes)
    own_sum = x_blocks[0]
    for s in shift_order:
        own_sum = own_sum + lax.ppermute(x_blocks[s], "x", [(src, (src + s) % nx) for src in range(nx)])
    weight_grad = own_sum.reshape(slot_dev, blk * blk)

    dense_w = jnp.where(
        has_tile.reshape(-1)[:, None, None], gathered[dense_rows], jnp.zeros((), gathered.dtype)
    ).reshape(panel_list, ncol, half, lanes)
    normed_grad = jnp.einsum("cthl,pcrl->tprh", expand, dense_w, preferred_element_type=jnp.float32)
    normed_grad = normed_grad.reshape(tok_rows, width)

    scaled = gain_row[None, :] * normed_grad
    inner = jnp.sum(scaled * inputs_f, axis=1, keepdims=True) / width
    input_grad = (recip * scaled - inputs_f * recip**3 * inner).astype(jnp.bfloat16)
    handed = shifted(input_grad, "section", -1)
    return (handed[None], weight_grad[None])


def solution(mesh):
    sec, fs = mesh.devices.shape
    mesh = jax.sharding.Mesh(mesh.devices.reshape(sec, fs // 8, 4, 2), ("section",) + FS)
    placed = (
        P("section", FS, None),
        P("section", FS, None),
        P("section", None),
        P("section", FS, None),
        P("section", None, None),
        P("section", None),
        P("section", None),
    )
    return jax.shard_map(
        local,
        mesh=mesh,
        in_specs=placed,
        out_specs=(P("section", FS, None), P("section", FS, None)),
        check_vma=False,
    )
```
